256 devices in a mesh: lat: 16 (over y, x_hi, core), lon: 16 (over z, x_lo).
Axes of the slice: x: 4 (x_hi: 2, x_lo: 2; x = x_hi * 2 + x_lo), y: 4, z: 8, core: 2. Of those that a mesh axis runs over, the one named last changes fastest.
Arguments:
- inputs: bfloat16 [256, 512, 192], P('lat', 'lon'), may hold values from -6 to 6
- grad_out: bfloat16 [256, 512, 192], P('lat', 'lon'), may hold values from -6 to 6
- dw_kernel: float32 [2, 7, 7, 192], replicated, may hold values from -0.875 to 0.875
- dw_bias: float32 [2, 192], replicated, may hold values from -3 to 3
- ln_gain: float32 [2, 192], replicated, may hold values from 0.1 to 1.9
- ln_bias: float32 [2, 192], replicated, may hold values from -3 to 3
- w_up: bfloat16 [2, 192, 768], replicated, may hold values from -0.4375 to 0.4375
- b_up: float32 [2, 768], replicated, may hold values from -3 to 3
- w_down: bfloat16 [2, 768, 192], replicated, may hold values from -0.21875 to 0.21875
- b_down: float32 [2, 192], replicated, may hold values from -3 to 3
- layer_scale: float32 [2, 192], replicated, may hold values from 0.5 to 1.5
Outputs:
- grad_inputs: bfloat16 [256, 512, 192], P('lat', 'lon')
- grad_kernel: float32 [2, 7, 7, 192], replicated
- grad_dw_bias: float32 [2, 192], replicated
- grad_ln_gain: float32 [2, 192], replicated
- grad_ln_bias: float32 [2, 192], replicated
- grad_w_up: float32 [2, 192, 768], replicated
- grad_b_up: float32 [2, 768], replicated
- grad_w_down: float32 [2, 768, 192], replicated
- grad_b_down: float32 [2, 192], replicated
- grad_layer_scale: float32 [2, 192], replicated
The draws below stay inside these ranges and needn't reach their ends.
All inputs are finite; a program needn't handle non-finite values.
Results may differ from the reference program's by a relative error of at most 0.018.
Values may be sent and summed in bfloat16 or wider, within the bound.
No kernel may reach another device: no remote copies, remote signals or barrier semaphores. Data moves between devices by JAX's collectives and lax.ppermute only.
A program may use at most 64 MiB of HBM per device.

```python
import math
import jax
import jax.numpy as jnp
from jax import lax

C = 192
HID = 768
ROWS_DEV = 16
H = 256
W = 512


def block_levels(key, shape, cuts, low, largest):
    def one(dim, blocks):
        steps = jax.random.uniform(jax.random.fold_in(jax.random.fold_in(key, 6), dim), (blocks,), jnp.float32, low / len(cuts), largest / len(cuts))
        return jnp.repeat(jnp.exp(steps), shape[dim] // blocks).reshape((-1,) + (1,) * (len(shape) - dim - 1))

    level = one(*cuts[0])
    for cut in cuts[1:]:
        level = level * one(*cut)
    return level


def bell_draw(stream_key, dims, scale, limit, cuts=(), kind=jnp.bfloat16):
    array = jax.random.normal(stream_key, dims, jnp.float32) * scale
    if len(cuts) > 0:
        array = block_levels(stream_key, dims, cuts, -0.22, 0.18) * array
    return jnp.clip(array, min=-limit, max=limit).astype(kind)


def setup_inputs(seed: int = 0) -> dict:
    seeds = jax.random.split(jax.random.key(seed), 12)
    return {
        "inputs": bell_draw(seeds[0], (H, W, C), 1.0, 6.0, ((0, 16), (1, 16))),
        "grad_out": bell_draw(seeds[1], (H, W, C), 1.0, 6.0, ((0, 16), (1, 16))),
        "dw_kernel": bell_draw(seeds[2], (2, 7, 7, C), 49 ** -0.5, 0.875, (), jnp.float32),
        "dw_bias": bell_draw(seeds[3], (2, C), 0.5, 3.0, (), jnp.float32),
        "ln_gain": jnp.clip(1.0 + 0.18 * jax.random.normal(seeds[4], (2, C), jnp.float32), 0.1, 1.9),
        "ln_bias": bell_draw(seeds[5], (2, C), 0.5, 3.0, (), jnp.float32),
        "w_up": bell_draw(seeds[6], (2, C, HID), C ** -0.5, 0.4375),
        "b_up": bell_draw(seeds[7], (2, HID), 0.5, 3.0, (), jnp.float32),
        "w_down": bell_draw(seeds[8], (2, HID, C), HID ** -0.5, 0.21875),
        "b_down": bell_draw(seeds[9], (2, C), 0.5, 3.0, (), jnp.float32),
        "layer_scale": jnp.clip(jax.random.uniform(seeds[10], (2, C), jnp.float32, 0.5, 1.5), 0.5, 1.5),
    }


EPS = 1e-06
ROOT_TWO_PI = math.sqrt(2.0 / math.pi)
CUBIC = 0.044715

def gelu_pair(hidden):
    inner = ROOT_TWO_PI * (hidden + CUBIC * hidden * hidden * hidden)
    tanh_val = jnp.tanh(inner)
    value = 0.5 * hidden * (1.0 + tanh_val)
    slope = 0.5 * (1.0 + tanh_val) + 0.5 * hidden * (1.0 - tanh_val * tanh_val) * ROOT_TWO_PI * (1.0 + 3.0 * CUBIC * hidden * hidden)
    return (value, slope)

def depthwise(extended, kernel, row_count, col_count):
    total = jnp.zeros((row_count, col_count, extended.shape[2]), jnp.float32)
    for tap_row in range(7):
        for tap_col in range(7):
            window = extended[tap_row:tap_row + row_count, tap_col:tap_col + col_count].astype(jnp.float32)
            total = total + window * kernel[tap_row, tap_col]
    return total

def kernel_grad(grad_cells, extended, row_count, col_count):
    grad_float = grad_cells.astype(jnp.float32)
    rows_out = []
    for tap_row in range(7):
        row_terms = []
        for tap_col in range(7):
            window = extended[tap_row:tap_row + row_count, tap_col:tap_col + col_count].astype(jnp.float32)
            row_terms.append(lax.optimization_barrier(jnp.sum(grad_float * window, axis=(0, 1))))
        rows_out.append(jnp.stack(row_terms))
    return jnp.stack(rows_out)

def spread(extended_grad, kernel, row_count, col_count, at_north, at_south):
    row_ids = jnp.arange(row_count + 6)[:, None, None]
    north_mask = jnp.logical_and(at_north, row_ids < 3)
    south_mask = jnp.logical_and(at_south, row_ids >= row_count + 3)
    polar = jnp.logical_or(north_mask, south_mask)
    zeros = jnp.zeros_like(extended_grad)
    normal = jnp.where(polar, zeros, extended_grad)
    north_part = jnp.where(north_mask, extended_grad, zeros)
    south_part = jnp.where(south_mask, extended_grad, zeros)
    result = depthwise(normal, kernel[::-1, ::-1], row_count, col_count)
    upper = depthwise(north_part[0:9], kernel[:, ::-1], 3, col_count)
    lower = depthwise(south_part[row_count - 3:row_count + 6], kernel[:, ::-1], 3, col_count)
    result = result.at[0:3].add(upper)
    return result.at[row_count - 3:row_count].add(lower)

def cells_forward(conv_cells, params):
    gain, shift_ln, weight_up, bias_up, weight_down, bias_down, branch_scale = params
    ch_mean = lax.optimization_barrier(jnp.mean(conv_cells, axis=-1, keepdims=True))
    centred = conv_cells - ch_mean
    ch_var = lax.optimization_barrier(jnp.mean(centred * centred, axis=-1, keepdims=True))
    inv_std = lax.rsqrt(ch_var + EPS)
    normal_x = centred * inv_std
    normed = (normal_x * gain + shift_ln).astype(jnp.bfloat16)
    hidden = jnp.dot(normed, weight_up, preferred_element_type=jnp.float32) + bias_up
    value, slope = gelu_pair(hidden)
    activ = value.astype(jnp.bfloat16)
    branch = jnp.dot(activ, weight_down, preferred_element_type=jnp.float32) + bias_down
    return (normed, normal_x, inv_std, activ, slope, branch)

def cells_backward(upstream, saved, params):
    normed, normal_x, inv_std, activ, slope, branch = saved
    gain, shift_ln, weight_up, bias_up, weight_down, bias_down, branch_scale = params
    up_float = upstream.astype(jnp.float32)
    d_scale = lax.optimization_barrier(jnp.sum(up_float * branch, axis=0))
    grad_branch = (up_float * branch_scale).astype(jnp.bfloat16)
    d_bias_down = lax.optimization_barrier(jnp.sum(grad_branch.astype(jnp.float32), axis=0))
    d_weight_down = jnp.dot(activ.T, grad_branch, preferred_element_type=jnp.float32)
    grad_activ = jnp.dot(grad_branch, weight_down.T, preferred_element_type=jnp.float32)
    grad_hidden = (grad_activ * slope).astype(jnp.bfloat16)
    d_bias_up = lax.optimization_barrier(jnp.sum(grad_hidden.astype(jnp.float32), axis=0))
    d_weight_up = jnp.dot(normed.T, grad_hidden, preferred_element_type=jnp.float32)
    grad_normed = jnp.dot(grad_hidden, weight_up.T, preferred_element_type=jnp.float32)
    d_gain = lax.optimization_barrier(jnp.sum(grad_normed * normal_x, axis=0))
    d_shift = lax.optimization_barrier(jnp.sum(grad_normed, axis=0))
    scaled = grad_normed * gain
    grad_conv = inv_std * (scaled - lax.optimization_barrier(jnp.mean(scaled, axis=-1, keepdims=True)) - normal_x * lax.optimization_barrier(jnp.mean(scaled * normal_x, axis=-1, keepdims=True)))
    return (grad_conv.astype(jnp.bfloat16), (d_gain, d_shift, d_weight_up, d_bias_up, d_weight_down, d_bias_down, d_scale))

def extend(field):
    height, width = (field.shape[0], field.shape[1])
    upper = jnp.roll(field[0:3][::-1], width // 2, axis=1)
    lower = jnp.roll(field[height - 3:height][::-1], width // 2, axis=1)
    stacked = jnp.concatenate([upper, field, lower], axis=0)
    return jnp.concatenate([stacked[:, width - 3:], stacked, stacked[:, 0:3]], axis=1)

def reference(inputs, grad_out, dw_kernel, dw_bias, ln_gain, ln_bias, w_up, b_up, w_down, b_down, layer_scale):
    height, width, channels = inputs.shape
    hidden_width = w_up.shape[2]
    blocks = height // ROWS_DEV

    def params(index):
        return (ln_gain[index], ln_bias[index], w_up[index], b_up[index], w_down[index], b_down[index], layer_scale[index])

    def as_rows(field):
        return field.reshape(blocks, ROWS_DEV * width, channels)
    first_ext = extend(inputs)
    first_conv = depthwise(first_ext, dw_kernel[0], height, width) + dw_bias[0]

    def forward_rows(carry, pieces):
        input_rows, conv_rows = pieces
        saved = cells_forward(conv_rows, params(0))
        mixed = (input_rows.astype(jnp.float32) + layer_scale[0] * saved[5]).astype(jnp.bfloat16)
        return (carry, mixed)
    unused, middle = lax.scan(forward_rows, jnp.zeros((), jnp.float32), (as_rows(inputs), as_rows(first_conv)))
    middle = middle.reshape(height, width, channels)
    second_ext = extend(middle)
    second_conv = depthwise(second_ext, dw_kernel[1], height, width) + dw_bias[1]

    def backward_block(index, upstream, conv_out, extended):

        def back_rows(totals, pieces):
            grad_rows, conv_rows = pieces
            saved = cells_forward(conv_rows, params(index))
            grad_cells, terms = cells_backward(grad_rows, saved, params(index))
            return (jax.tree.map(lambda left, right: left + right, totals, terms), grad_cells)
        start = (jnp.zeros((channels,), jnp.float32), jnp.zeros((channels,), jnp.float32), jnp.zeros((channels, hidden_width), jnp.float32), jnp.zeros((hidden_width,), jnp.float32), jnp.zeros((hidden_width, channels), jnp.float32), jnp.zeros((channels,), jnp.float32), jnp.zeros((channels,), jnp.float32))
        totals, grad_cells = lax.scan(back_rows, start, (as_rows(upstream), as_rows(conv_out)))
        grad_cells = grad_cells.reshape(height, width, channels)
        kernel_term = kernel_grad(grad_cells, extended, height, width)
        bias_term = lax.optimization_barrier(jnp.sum(grad_cells.astype(jnp.float32), axis=(0, 1)))
        back = spread(extend(grad_cells), dw_kernel[index], height, width, True, True)
        return (back, (kernel_term, bias_term) + totals)
    back_second, grads_second = backward_block(1, grad_out, second_conv, second_ext)
    upstream_first = (grad_out.astype(jnp.float32) + back_second).astype(jnp.bfloat16)
    back_first, grads_first = backward_block(0, upstream_first, first_conv, first_ext)
    grad_inputs = (upstream_first.astype(jnp.float32) + back_first).astype(jnp.bfloat16)
    inv_root = 1.0 / math.sqrt(height * width)
    joined = [jnp.stack([grads_first[slot], grads_second[slot]]) * inv_root for slot in range(9)]
    return (grad_inputs, joined[0], joined[1], joined[2], joined[3], joined[4], joined[5], joined[6], joined[7], joined[8])
```

```python
import math

import jax
import jax.numpy as jnp
from jax import lax
from jax.sharding import PartitionSpec as P

EPS = 1e-06
ROOT_TWO_PI = math.sqrt(2.0 / math.pi)
CUBIC = 0.044715


def with_halo(cells, sides, width, closed):
    for axis, dim in sides:
        count = lax.axis_size(axis)
        ends = count if closed else count - 1
        head = lax.slice_in_dim(cells, 0, width, axis=dim)
        tail = lax.slice_in_dim(cells, cells.shape[dim] - width, cells.shape[dim], axis=dim)
        cells = jnp.concatenate(
            [
                lax.ppermute(tail, axis, [(i, (i + 1) % count) for i in range(ends)]),
                cells,
                lax.ppermute(head, axis, [((i + 1) % count, i) for i in range(ends)]),
            ],
            axis=dim,
        )
    return cells


def from_behind(block, axis, distance):
    devices = range(lax.axis_size(axis))
    route = [((i - distance) % len(devices), i) for i in devices]
    return lax.ppermute(block, axis, route)


def gelu_pair(hidden):
    inner = ROOT_TWO_PI * (hidden + CUBIC * hidden * hidden * hidden)
    tanh_val = jnp.tanh(inner)
    value = 0.5 * hidden * (1.0 + tanh_val)
    slope = 0.5 * (1.0 + tanh_val) + 0.5 * hidden * (1.0 - tanh_val * tanh_val) * ROOT_TWO_PI * (
        1.0 + 3.0 * CUBIC * hidden * hidden
    )
    return (value, slope)


def depthwise(extended, kernel, row_count, col_count):
    total = jnp.zeros((row_count, col_count, extended.shape[2]), jnp.float32)
    for tap_row in range(7):
        for tap_col in range(7):
            window = extended[tap_row : tap_row + row_count, tap_col : tap_col + col_count].astype(
                jnp.float32
            )
            total = total + window * kernel[tap_row, tap_col]
    return total


def kernel_grad(grad_cells, extended, row_count, col_count):
    grad_float = grad_cells.astype(jnp.float32)
    rows_out = []
    for tap_row in range(7):
        row_terms = []
        for tap_col in range(7):
            window = extended[tap_row : tap_row + row_count, tap_col : tap_col + col_count].astype(
                jnp.float32
            )
            row_terms.append(jnp.sum(grad_float * window, axis=(0, 1)))
        rows_out.append(jnp.stack(row_terms))
    return jnp.stack(rows_out)


def spread(extended_grad, kernel, row_count, col_count, at_north, at_south):
    row_ids = jnp.arange(row_count + 6)[:, None, None]
    north_mask = jnp.logical_and(at_north, row_ids < 3)
    south_mask = jnp.logical_and(at_south, row_ids >= row_count + 3)
    polar = jnp.logical_or(north_mask, south_mask)
    zeros = jnp.zeros_like(extended_grad)
    normal = jnp.where(polar, zeros, extended_grad)
    north_part = jnp.where(north_mask, extended_grad, zeros)
    south_part = jnp.where(south_mask, extended_grad, zeros)
    result = depthwise(normal, kernel[::-1, ::-1], row_count, col_count)
    upper = depthwise(north_part[0:9], kernel[:, ::-1], 3, col_count)
    lower = depthwise(south_part[row_count - 3 : row_count + 6], kernel[:, ::-1], 3, col_count)
    result = result.at[0:3].add(upper)
    return result.at[row_count - 3 : row_count].add(lower)


def cells_forward(conv_cells, params):
    gain, shift_ln, weight_up, bias_up, weight_down, bias_down, branch_scale = params
    ch_mean = jnp.mean(conv_cells, axis=-1, keepdims=True)
    centred = conv_cells - ch_mean
    ch_var = jnp.mean(centred * centred, axis=-1, keepdims=True)
    inv_std = lax.rsqrt(ch_var + EPS)
    normal_x = centred * inv_std
    normed = (normal_x * gain + shift_ln).astype(jnp.bfloat16)
    hidden = jnp.dot(normed, weight_up, preferred_element_type=jnp.float32) + bias_up
    value, slope = gelu_pair(hidden)
    activ = value.astype(jnp.bfloat16)
    branch = jnp.dot(activ, weight_down, preferred_element_type=jnp.float32) + bias_down
    return (normed, normal_x, inv_std, activ, slope, branch)


def cells_backward(upstream, saved, params):
    normed, normal_x, inv_std, activ, slope, branch = saved
    gain, shift_ln, weight_up, bias_up, weight_down, bias_down, branch_scale = params
    up_float = upstream.astype(jnp.float32)
    d_scale = jnp.sum(up_float * branch, axis=0)
    grad_branch = (up_float * branch_scale).astype(jnp.bfloat16)
    d_bias_down = jnp.sum(grad_branch.astype(jnp.float32), axis=0)
    d_weight_down = jnp.dot(grad_branch.T, activ, preferred_element_type=jnp.float32)
    grad_activ = jnp.dot(grad_branch, weight_down.T, preferred_element_type=jnp.float32)
    grad_hidden = (grad_activ * slope).astype(jnp.bfloat16)
    d_bias_up = jnp.sum(grad_hidden.astype(jnp.float32), axis=0)
    d_weight_up = jnp.dot(normed.T, grad_hidden, preferred_element_type=jnp.float32)
    grad_normed = jnp.dot(grad_hidden, weight_up.T, preferred_element_type=jnp.float32)
    d_gain = jnp.sum(grad_normed * normal_x, axis=0)
    d_shift = jnp.sum(grad_normed, axis=0)
    scaled = grad_normed * gain
    grad_conv = inv_std * (
        scaled
        - jnp.mean(scaled, axis=-1, keepdims=True)
        - normal_x * jnp.mean(scaled * normal_x, axis=-1, keepdims=True)
    )
    return (
        grad_conv.astype(jnp.bfloat16),
        (d_gain, d_shift, d_weight_up, d_bias_up, d_weight_down, d_bias_down, d_scale),
    )


def extend(field, at_north, at_south):
    row_count = field.shape[0]
    lat_ext = with_halo(field, (("lat", 0),), 3, False)
    edge_rows = jnp.where(at_north, field[0:3], field[row_count - 3 : row_count])
    across = from_behind(edge_rows, "lon", lax.axis_size("lon") // 2)[::-1]
    upper = jnp.where(at_north, across, lat_ext[0:3])
    lower = jnp.where(at_south, across, lat_ext[row_count + 3 : row_count + 6])
    stacked = jnp.concatenate([upper, lat_ext[3 : row_count + 3], lower], axis=0)
    return with_halo(stacked, (("lon", 1),), 3, True)


HALVING_ORDER = (("lat", 0), ("lon", 0), ("lon", 1), ("lat", 2), ("lat", 1), ("lon", 2), ("lat", 3), ("lon", 3))


def xor_partners(axis, bit):
    return [(j, j ^ (1 << bit)) for j in range(lax.axis_size(axis))]


def halving_sum(buf):
    steps = []
    for axis, bit in HALVING_ORDER:
        side = (lax.axis_index(axis) >> bit) & 1
        dim = 0 if buf.shape[0] % 2 == 0 and len(steps) < 5 else 1
        half = buf.shape[dim] // 2
        send = lax.dynamic_slice_in_dim(buf, (1 - side) * half, half, axis=dim)
        keep = lax.dynamic_slice_in_dim(buf, side * half, half, axis=dim)
        buf = keep + lax.ppermute(send, axis, xor_partners(axis, bit))
        steps.append((axis, bit, side, dim))
    for axis, bit, side, dim in reversed(steps):
        other = lax.ppermute(buf, axis, xor_partners(axis, bit))
        low = jnp.where(side == 0, buf, other)
        high = jnp.where(side == 0, other, buf)
        buf = jnp.concatenate([low, high], axis=dim)
    return buf


def pack_terms(first, second):
    width = first[4].shape[1]
    big = jnp.concatenate([first[4], second[4], first[6], second[6]], axis=0)
    small = [piece.reshape(-1) for grads in (first, second) for i, piece in enumerate(grads) if i not in (4, 6)]
    flat = jnp.concatenate(small)
    rows = 32
    flat = jnp.pad(flat, (0, rows * width - flat.shape[0]))
    return jnp.concatenate([big, flat.reshape(rows, width)], axis=0)


def unpack_terms(buf, first, second):
    size = first[4].shape[0]
    big = buf[: 4 * size]
    flat = buf[4 * size :].reshape(-1)
    out = []
    offset = 0
    for b, grads in enumerate((first, second)):
        pieces = []
        for i, piece in enumerate(grads):
            if i == 4:
                pieces.append(big[b * size : (b + 1) * size])
            elif i == 6:
                pieces.append(big[(2 + b) * size : (3 + b) * size].T)
            else:
                pieces.append(flat[offset : offset + piece.size].reshape(piece.shape))
                offset = offset + piece.size
        out.append(tuple(pieces))
    return out


def per_device(
    inputs, grad_out, dw_kernel, dw_bias, ln_gain, ln_bias, w_up, b_up, w_down, b_down, layer_scale
):
    row_count, col_count, channels = inputs.shape
    at_north = lax.axis_index("lat") == 0
    at_south = lax.axis_index("lat") == lax.axis_size("lat") - 1
    cell_total = row_count * lax.axis_size("lat") * col_count * lax.axis_size("lon")

    def params(index):
        return (
            ln_gain[index],
            ln_bias[index],
            w_up[index],
            b_up[index],
            w_down[index],
            b_down[index],
            layer_scale[index],
        )

    def forward_block(index, field):
        extended = extend(field, at_north, at_south)
        conv_out = depthwise(extended, dw_kernel[index], row_count, col_count) + dw_bias[index]
        saved = cells_forward(conv_out.reshape(-1, channels), params(index))
        return (extended, saved)

    def backward_block(index, upstream, saved, extended):
        grad_cells, terms = cells_backward(upstream.reshape(-1, channels), saved, params(index))
        grad_cells = grad_cells.reshape(row_count, col_count, channels)
        kernel_term = kernel_grad(grad_cells, extended, row_count, col_count)
        bias_term = jnp.sum(grad_cells.astype(jnp.float32), axis=(0, 1))
        back = spread(
            extend(grad_cells, at_north, at_south),
            dw_kernel[index],
            row_count,
            col_count,
            at_north,
            at_south,
        )
        return (back, (kernel_term, bias_term) + terms)

    first_ext, first_saved = forward_block(0, inputs)
    middle = (
        inputs.reshape(-1, channels).astype(jnp.float32) + layer_scale[0] * first_saved[5]
    ).astype(jnp.bfloat16)
    middle = middle.reshape(row_count, col_count, channels)
    second_ext, second_saved = forward_block(1, middle)
    back_second, grads_second = backward_block(1, grad_out, second_saved, second_ext)
    upstream_first = (grad_out.astype(jnp.float32) + back_second).astype(jnp.bfloat16)
    back_first, grads_first = backward_block(0, upstream_first, first_saved, first_ext)
    grad_inputs = (upstream_first.astype(jnp.float32) + back_first).astype(jnp.bfloat16)
    summed = halving_sum(pack_terms(grads_first, grads_second))
    grads_first, grads_second = unpack_terms(summed, grads_first, grads_second)
    inv_root = 1.0 / math.sqrt(cell_total)
    joined = [jnp.stack([grads_first[slot], grads_second[slot]]) * inv_root for slot in range(9)]
    return (
        grad_inputs,
        joined[0],
        joined[1],
        joined[2],
        joined[3],
        joined[4],
        joined[5],
        joined[6],
        joined[7],
        joined[8],
    )


def solution(mesh):
    placed = (
        P("lat", "lon", None),
        P("lat", "lon", None),
        P(),
        P(),
        P(),
        P(),
        P(),
        P(),
        P(),
        P(),
        P(),
    )
    return jax.shard_map(
        per_device,
        mesh=mesh,
        in_specs=placed,
        out_specs=(P("lat", "lon", None), P(), P(), P(), P(), P(), P(), P(), P(), P()),
        check_vma=False,
    )
```

```python
import math

import jax
import jax.numpy as jnp
from jax import lax
from jax.sharding import PartitionSpec as P

EPS = 1e-06
ROOT_TWO_PI = math.sqrt(2.0 / math.pi)
CUBIC = 0.044715


def with_halo(cells, sides, width, closed):
    for axis, dim in sides:
        count = lax.axis_size(axis)
        ends = count if closed else count - 1
        head = lax.slice_in_dim(cells, 0, width, axis=dim)
        tail = lax.slice_in_dim(cells, cells.shape[dim] - width, cells.shape[dim], axis=dim)
        cells = jnp.concatenate(
            [
                lax.ppermute(tail, axis, [(i, (i + 1) % count) for i in range(ends)]),
                cells,
                lax.ppermute(head, axis, [((i + 1) % count, i) for i in range(ends)]),
            ],
            axis=dim,
        )
    return cells


def from_behind(block, axis, distance):
    devices = range(lax.axis_size(axis))
    route = [((i - distance) % len(devices), i) for i in devices]
    return lax.ppermute(block, axis, route)


def gelu_pair(hidden):
    inner = ROOT_TWO_PI * (hidden + CUBIC * hidden * hidden * hidden)
    tanh_val = jnp.tanh(inner)
    value = 0.5 * hidden * (1.0 + tanh_val)
    slope = 0.5 * (1.0 + tanh_val) + 0.5 * hidden * (1.0 - tanh_val * tanh_val) * ROOT_TWO_PI * (
        1.0 + 3.0 * CUBIC * hidden * hidden
    )
    return (value, slope)


def depthwise(extended, kernel, row_count, col_count):
    total = jnp.zeros((row_count, col_count, extended.shape[2]), jnp.float32)
    for tap_row in range(7):
        for tap_col in range(7):
            window = extended[tap_row : tap_row + row_count, tap_col : tap_col + col_count].astype(
                jnp.float32
            )
            total = total + window * kernel[tap_row, tap_col]
    return total


def kernel_grad(grad_cells, extended, row_count, col_count):
    grad_float = grad_cells.astype(jnp.float32)
    rows_out = []
    for tap_row in range(7):
        row_terms = []
        for tap_col in range(7):
            window = extended[tap_row : tap_row + row_count, tap_col : tap_col + col_count].astype(
                jnp.float32
            )
            row_terms.append(jnp.sum(grad_float * window, axis=(0, 1)))
        rows_out.append(jnp.stack(row_terms))
    return jnp.stack(rows_out)


def spread(extended_grad, kernel, row_count, col_count, at_north, at_south):
    row_ids = jnp.arange(row_count + 6)[:, None, None]
    north_mask = jnp.logical_and(at_north, row_ids < 3)
    south_mask = jnp.logical_and(at_south, row_ids >= row_count + 3)
    polar = jnp.logical_or(north_mask, south_mask)
    zeros = jnp.zeros_like(extended_grad)
    normal = jnp.where(polar, zeros, extended_grad)
    north_part = jnp.where(north_mask, extended_grad, zeros)
    south_part = jnp.where(south_mask, extended_grad, zeros)
    result = depthwise(normal, kernel[::-1, ::-1], row_count, col_count)
    upper = depthwise(north_part[0:9], kernel[:, ::-1], 3, col_count)
    lower = depthwise(south_part[row_count - 3 : row_count + 6], kernel[:, ::-1], 3, col_count)
    result = result.at[0:3].add(upper)
    return result.at[row_count - 3 : row_count].add(lower)


def cells_forward(conv_cells, params):
    gain, shift_ln, weight_up, bias_up, weight_down, bias_down, branch_scale = params
    ch_mean = jnp.mean(conv_cells, axis=-1, keepdims=True)
    centred = conv_cells - ch_mean
    ch_var = jnp.mean(centred * centred, axis=-1, keepdims=True)
    inv_std = lax.rsqrt(ch_var + EPS)
    normal_x = centred * inv_std
    normed = (normal_x * gain + shift_ln).astype(jnp.bfloat16)
    hidden = jnp.dot(normed, weight_up, preferred_element_type=jnp.float32) + bias_up
    value, slope = gelu_pair(hidden)
    activ = value.astype(jnp.bfloat16)
    branch = jnp.dot(activ, weight_down, preferred_element_type=jnp.float32) + bias_down
    return (normed, normal_x, inv_std, activ, slope, branch)


def cells_backward(upstream, saved, params):
    normed, normal_x, inv_std, activ, slope, branch = saved
    gain, shift_ln, weight_up, bias_up, weight_down, bias_down, branch_scale = params
    up_float = upstream.astype(jnp.float32)
    d_scale = jnp.sum(up_float * branch, axis=0)
    grad_branch = (up_float * branch_scale).astype(jnp.bfloat16)
    d_bias_down = jnp.sum(grad_branch.astype(jnp.float32), axis=0)
    d_weight_down = jnp.dot(grad_branch.T, activ, preferred_element_type=jnp.float32)
    grad_activ = jnp.dot(grad_branch, weight_down.T, preferred_element_type=jnp.float32)
    grad_hidden = (grad_activ * slope).astype(jnp.bfloat16)
    d_bias_up = jnp.sum(grad_hidden.astype(jnp.float32), axis=0)
    d_weight_up = jnp.dot(normed.T, grad_hidden, preferred_element_type=jnp.float32)
    grad_normed = jnp.dot(grad_hidden, weight_up.T, preferred_element_type=jnp.float32)
    d_gain = jnp.sum(grad_normed * normal_x, axis=0)
    d_shift = jnp.sum(grad_normed, axis=0)
    scaled = grad_normed * gain
    grad_conv = inv_std * (
        scaled
        - jnp.mean(scaled, axis=-1, keepdims=True)
        - normal_x * jnp.mean(scaled * normal_x, axis=-1, keepdims=True)
    )
    return (
        grad_conv.astype(jnp.bfloat16),
        (d_gain, d_shift, d_weight_up, d_bias_up, d_weight_down, d_bias_down, d_scale),
    )


def extend(field, at_north, at_south):
    row_count = field.shape[0]
    lat_ext = with_halo(field, (("lat", 0),), 3, False)
    edge_rows = jnp.where(at_north, field[0:3], field[row_count - 3 : row_count])
    across = from_behind(edge_rows, "lon", lax.axis_size("lon") // 2)[::-1]
    upper = jnp.where(at_north, across, lat_ext[0:3])
    lower = jnp.where(at_south, across, lat_ext[row_count + 3 : row_count + 6])
    stacked = jnp.concatenate([upper, lat_ext[3 : row_count + 3], lower], axis=0)
    return with_halo(stacked, (("lon", 1),), 3, True)


HALVING_ORDER = (("lat", 0), ("lon", 0), ("lon", 1), ("lat", 2), ("lat", 1), ("lon", 2), ("lat", 3), ("lon", 3))


def xor_partners(axis, bit):
    return [(j, j ^ (1 << bit)) for j in range(lax.axis_size(axis))]


def halving_sum(buf, hooks):
    steps = []
    for axis, bit in HALVING_ORDER:
        if len(steps) in hooks:
            buf = hooks[len(steps)](buf)
        side = (lax.axis_index(axis) >> bit) & 1
        dim = 0 if buf.shape[0] % 2 == 0 and len(steps) < 5 else 1
        half = buf.shape[dim] // 2
        send = lax.dynamic_slice_in_dim(buf, (1 - side) * half, half, axis=dim)
        keep = lax.dynamic_slice_in_dim(buf, side * half, half, axis=dim)
        buf = keep + lax.ppermute(send, axis, xor_partners(axis, bit))
        steps.append((axis, bit, side, dim))
    for axis, bit, side, dim in reversed(steps):
        other = lax.ppermute(buf, axis, xor_partners(axis, bit))
        low = jnp.where(side == 0, buf, other)
        high = jnp.where(side == 0, other, buf)
        buf = jnp.concatenate([low, high], axis=dim)
    return buf


def pack_terms(first, second):
    width = first[4].shape[1]
    big = jnp.concatenate([first[4], second[4], first[6], second[6]], axis=0)
    small = [piece.reshape(-1) for grads in (first, second) for i, piece in enumerate(grads) if i not in (4, 6)]
    flat = jnp.concatenate(small)
    rows = 32
    flat = jnp.pad(flat, (0, rows * width - flat.shape[0]))
    return jnp.concatenate([big, flat.reshape(rows, width)], axis=0)


def unpack_terms(buf, first, second):
    size = first[4].shape[0]
    big = buf[: 4 * size]
    flat = buf[4 * size :].reshape(-1)
    out = []
    offset = 0
    for b, grads in enumerate((first, second)):
        pieces = []
        for i, piece in enumerate(grads):
            if i == 4:
                pieces.append(big[b * size : (b + 1) * size])
            elif i == 6:
                pieces.append(big[(2 + b) * size : (3 + b) * size].T)
            else:
                pieces.append(flat[offset : offset + piece.size].reshape(piece.shape))
                offset = offset + piece.size
        out.append(tuple(pieces))
    return out


def per_device(
    inputs, grad_out, dw_kernel, dw_bias, ln_gain, ln_bias, w_up, b_up, w_down, b_down, layer_scale
):
    row_count, col_count, channels = inputs.shape
    at_north = lax.axis_index("lat") == 0
    at_south = lax.axis_index("lat") == lax.axis_size("lat") - 1
    cell_total = row_count * lax.axis_size("lat") * col_count * lax.axis_size("lon")

    def params(index):
        return (
            ln_gain[index],
            ln_bias[index],
            w_up[index],
            b_up[index],
            w_down[index],
            b_down[index],
            layer_scale[index],
        )

    def forward_block(index, field):
        extended = extend(field, at_north, at_south)
        conv_out = depthwise(extended, dw_kernel[index], row_count, col_count) + dw_bias[index]
        saved = cells_forward(conv_out.reshape(-1, channels), params(index))
        return (extended, saved)

    def backward_cells(index, upstream, saved, extended):
        grad_cells, terms = cells_backward(upstream.reshape(-1, channels), saved, params(index))
        grad_cells = grad_cells.reshape(row_count, col_count, channels)
        kernel_term = kernel_grad(grad_cells, extended, row_count, col_count)
        bias_term = jnp.sum(grad_cells.astype(jnp.float32), axis=(0, 1))
        return grad_cells, (kernel_term, bias_term) + terms

    def backward_block(index, upstream, saved, extended):
        grad_cells, terms = backward_cells(index, upstream, saved, extended)
        back = spread(
            extend(grad_cells, at_north, at_south),
            dw_kernel[index],
            row_count,
            col_count,
            at_north,
            at_south,
        )
        return (back, terms)

    first_ext, first_saved = forward_block(0, inputs)
    middle = (
        inputs.reshape(-1, channels).astype(jnp.float32) + layer_scale[0] * first_saved[5]
    ).astype(jnp.bfloat16)
    middle = middle.reshape(row_count, col_count, channels)
    second_ext, second_saved = forward_block(1, middle)
    back_second, grads_second = backward_block(1, grad_out, second_saved, second_ext)
    upstream_first = (grad_out.astype(jnp.float32) + back_second).astype(jnp.bfloat16)
    grad_cells_first, grads_first = backward_cells(0, upstream_first, first_saved, first_ext)
    pending = {"ext": extend(grad_cells_first, at_north, at_south)}

    def tie_extension(buf):
        buf, ext = lax.optimization_barrier((buf, pending["ext"]))
        pending["back"] = spread(ext, dw_kernel[0], row_count, col_count, at_north, at_south)
        return buf

    def tie_back(buf):
        buf, pending["back"] = lax.optimization_barrier((buf, pending["back"]))
        return buf

    summed = halving_sum(pack_terms(grads_first, grads_second), {2: tie_extension, 7: tie_back})
    grads_first, grads_second = unpack_terms(summed, grads_first, grads_second)
    grad_inputs = (upstream_first.astype(jnp.float32) + pending["back"]).astype(jnp.bfloat16)
    inv_root = 1.0 / math.sqrt(cell_total)
    joined = [jnp.stack([grads_first[slot], grads_second[slot]]) * inv_root for slot in range(9)]
    return (
        grad_inputs,
        joined[0],
        joined[1],
        joined[2],
        joined[3],
        joined[4],
        joined[5],
        joined[6],
        joined[7],
        joined[8],
    )


def solution(mesh):
    placed = (
        P("lat", "lon", None),
        P("lat", "lon", None),
        P(),
        P(),
        P(),
        P(),
        P(),
        P(),
        P(),
        P(),
        P(),
    )
    return jax.shard_map(
        per_device,
        mesh=mesh,
        in_specs=placed,
        out_specs=(P("lat", "lon", None), P(), P(), P(), P(), P(), P(), P(), P(), P()),
        check_vma=False,
    )
```

```python
import math

import jax
import jax.numpy as jnp
from jax import lax
from jax.sharding import PartitionSpec as P

EPS = 1e-06
ROOT_TWO_PI = math.sqrt(2.0 / math.pi)
CUBIC = 0.044715


def with_halo(cells, sides, width, closed):
    for axis, dim in sides:
        count = lax.axis_size(axis)
        ends = count if closed else count - 1
        head = lax.slice_in_dim(cells, 0, width, axis=dim)
        tail = lax.slice_in_dim(cells, cells.shape[dim] - width, cells.shape[dim], axis=dim)
        cells = jnp.concatenate(
            [
                lax.ppermute(tail, axis, [(i, (i + 1) % count) for i in range(ends)]),
                cells,
                lax.ppermute(head, axis, [((i + 1) % count, i) for i in range(ends)]),
            ],
            axis=dim,
        )
    return cells


def from_behind(block, axis, distance):
    devices = range(lax.axis_size(axis))
    route = [((i - distance) % len(devices), i) for i in devices]
    return lax.ppermute(block, axis, route)


def gelu_pair(hidden):
    inner = ROOT_TWO_PI * (hidden + CUBIC * hidden * hidden * hidden)
    tanh_val = jnp.tanh(inner)
    value = 0.5 * hidden * (1.0 + tanh_val)
    slope = 0.5 * (1.0 + tanh_val) + 0.5 * hidden * (1.0 - tanh_val * tanh_val) * ROOT_TWO_PI * (
        1.0 + 3.0 * CUBIC * hidden * hidden
    )
    return (value, slope)


def depthwise(extended, kernel, row_count, col_count):
    total = jnp.zeros((row_count, col_count, extended.shape[2]), jnp.float32)
    for tap_row in range(7):
        for tap_col in range(7):
            window = extended[tap_row : tap_row + row_count, tap_col : tap_col + col_count].astype(
                jnp.float32
            )
            total = total + window * kernel[tap_row, tap_col]
    return total


def kernel_grad(grad_cells, extended, row_count, col_count):
    grad_float = grad_cells.astype(jnp.float32)
    rows_out = []
    for tap_row in range(7):
        row_terms = []
        for tap_col in range(7):
            window = extended[tap_row : tap_row + row_count, tap_col : tap_col + col_count].astype(
                jnp.float32
            )
            row_terms.append(jnp.sum(grad_float * window, axis=(0, 1)))
        rows_out.append(jnp.stack(row_terms))
    return jnp.stack(rows_out)


def spread(extended_grad, kernel, row_count, col_count, at_north, at_south):
    row_ids = jnp.arange(row_count + 6)[:, None, None]
    north_mask = jnp.logical_and(at_north, row_ids < 3)
    south_mask = jnp.logical_and(at_south, row_ids >= row_count + 3)
    polar = jnp.logical_or(north_mask, south_mask)
    zeros = jnp.zeros_like(extended_grad)
    normal = jnp.where(polar, zeros, extended_grad)
    north_part = jnp.where(north_mask, extended_grad, zeros)
    south_part = jnp.where(south_mask, extended_grad, zeros)
    result = depthwise(normal, kernel[::-1, ::-1], row_count, col_count)
    upper = depthwise(north_part[0:9], kernel[:, ::-1], 3, col_count)
    lower = depthwise(south_part[row_count - 3 : row_count + 6], kernel[:, ::-1], 3, col_count)
    result = result.at[0:3].add(upper)
    return result.at[row_count - 3 : row_count].add(lower)


def cells_forward(conv_cells, params):
    gain, shift_ln, weight_up, bias_up, weight_down, bias_down, branch_scale = params
    ch_mean = jnp.mean(conv_cells, axis=-1, keepdims=True)
    centred = conv_cells - ch_mean
    ch_var = jnp.mean(centred * centred, axis=-1, keepdims=True)
    inv_std = lax.rsqrt(ch_var + EPS)
    normal_x = centred * inv_std
    normed = (normal_x * gain + shift_ln).astype(jnp.bfloat16)
    hidden = jnp.dot(normed, weight_up, preferred_element_type=jnp.float32) + bias_up
    value, slope = gelu_pair(hidden)
    activ = value.astype(jnp.bfloat16)
    branch = jnp.dot(activ, weight_down, preferred_element_type=jnp.float32) + bias_down
    return (normed, normal_x, inv_std, activ, slope, branch)


def cells_backward(upstream, saved, params):
    normed, normal_x, inv_std, activ, slope, branch = saved
    gain, shift_ln, weight_up, bias_up, weight_down, bias_down, branch_scale = params
    up_float = upstream.astype(jnp.float32)
    d_scale = jnp.sum(up_float * branch, axis=0)
    grad_branch = (up_float * branch_scale).astype(jnp.bfloat16)
    d_bias_down = jnp.sum(grad_branch.astype(jnp.float32), axis=0)
    d_weight_down = jnp.dot(grad_branch.T, activ, preferred_element_type=jnp.float32)
    grad_activ = jnp.dot(grad_branch, weight_down.T, preferred_element_type=jnp.float32)
    grad_hidden = (grad_activ * slope).astype(jnp.bfloat16)
    d_bias_up = jnp.sum(grad_hidden.astype(jnp.float32), axis=0)
    d_weight_up = jnp.dot(normed.T, grad_hidden, preferred_element_type=jnp.float32)
    grad_normed = jnp.dot(grad_hidden, weight_up.T, preferred_element_type=jnp.float32)
    d_gain = jnp.sum(grad_normed * normal_x, axis=0)
    d_shift = jnp.sum(grad_normed, axis=0)
    scaled = grad_normed * gain
    grad_conv = inv_std * (
        scaled
        - jnp.mean(scaled, axis=-1, keepdims=True)
        - normal_x * jnp.mean(scaled * normal_x, axis=-1, keepdims=True)
    )
    return (
        grad_conv.astype(jnp.bfloat16),
        (d_gain, d_shift, d_weight_up, d_bias_up, d_weight_down, d_bias_down, d_scale),
    )


def extend(field, at_north, at_south):
    row_count = field.shape[0]
    lat_ext = with_halo(field, (("lat", 0),), 3, False)
    edge_rows = jnp.where(at_north, field[0:3], field[row_count - 3 : row_count])
    across = from_behind(edge_rows, "lon", lax.axis_size("lon") // 2)[::-1]
    upper = jnp.where(at_north, across, lat_ext[0:3])
    lower = jnp.where(at_south, across, lat_ext[row_count + 3 : row_count + 6])
    stacked = jnp.concatenate([upper, lat_ext[3 : row_count + 3], lower], axis=0)
    return with_halo(stacked, (("lon", 1),), 3, True)


HALVING_ORDER = (("lat", 0), ("lon", 0), ("lon", 1), ("lat", 2), ("lat", 1), ("lon", 2), ("lat", 3), ("lon", 3))


def xor_partners(axis, bit):
    return [(j, j ^ (1 << bit)) for j in range(lax.axis_size(axis))]


def halving_sum(buf, halvings=5):
    steps = []
    for axis, bit in HALVING_ORDER[:halvings]:
        side = (lax.axis_index(axis) >> bit) & 1
        half = buf.shape[0] // 2
        send = lax.dynamic_slice_in_dim(buf, (1 - side) * half, half, axis=0)
        keep = lax.dynamic_slice_in_dim(buf, side * half, half, axis=0)
        buf = keep + lax.ppermute(send, axis, xor_partners(axis, bit))
        steps.append((axis, bit, side))
    for axis, bit in HALVING_ORDER[halvings:]:
        buf = buf + lax.ppermute(buf, axis, xor_partners(axis, bit))
    buf = buf.astype(jnp.bfloat16)
    for axis, bit, side in reversed(steps):
        other = lax.ppermute(buf, axis, xor_partners(axis, bit))
        low = jnp.where(side == 0, buf, other)
        high = jnp.where(side == 0, other, buf)
        buf = jnp.concatenate([low, high], axis=0)
    return buf.astype(jnp.float32)


def pack_terms(first, second):
    width = first[4].shape[1]
    big = jnp.concatenate([first[4], second[4], first[6], second[6]], axis=0)
    small = [piece.reshape(-1) for grads in (first, second) for i, piece in enumerate(grads) if i not in (4, 6)]
    flat = jnp.concatenate(small)
    rows = 32
    flat = jnp.pad(flat, (0, rows * width - flat.shape[0]))
    return jnp.concatenate([big, flat.reshape(rows, width)], axis=0)


def unpack_terms(buf, first, second):
    size = first[4].shape[0]
    big = buf[: 4 * size]
    flat = buf[4 * size :].reshape(-1)
    out = []
    offset = 0
    for b, grads in enumerate((first, second)):
        pieces = []
        for i, piece in enumerate(grads):
            if i == 4:
                pieces.append(big[b * size : (b + 1) * size])
            elif i == 6:
                pieces.append(big[(2 + b) * size : (3 + b) * size].T)
            else:
                pieces.append(flat[offset : offset + piece.size].reshape(piece.shape))
                offset = offset + piece.size
        out.append(tuple(pieces))
    return out


def per_device(
    inputs, grad_out, dw_kernel, dw_bias, ln_gain, ln_bias, w_up, b_up, w_down, b_down, layer_scale
):
    row_count, col_count, channels = inputs.shape
    at_north = lax.axis_index("lat") == 0
    at_south = lax.axis_index("lat") == lax.axis_size("lat") - 1
    cell_total = row_count * lax.axis_size("lat") * col_count * lax.axis_size("lon")

    def params(index):
        return (
            ln_gain[index],
            ln_bias[index],
            w_up[index],
            b_up[index],
            w_down[index],
            b_down[index],
            layer_scale[index],
        )

    def forward_block(index, field):
        extended = extend(field, at_north, at_south)
        conv_out = depthwise(extended, dw_kernel[index], row_count, col_count) + dw_bias[index]
        saved = cells_forward(conv_out.reshape(-1, channels), params(index))
        return (extended, saved)

    def backward_block(index, upstream, saved, extended):
        grad_cells, terms = cells_backward(upstream.reshape(-1, channels), saved, params(index))
        grad_cells = grad_cells.reshape(row_count, col_count, channels)
        kernel_term = kernel_grad(grad_cells, extended, row_count, col_count)
        bias_term = jnp.sum(grad_cells.astype(jnp.float32), axis=(0, 1))
        back = spread(
            extend(grad_cells, at_north, at_south),
            dw_kernel[index],
            row_count,
            col_count,
            at_north,
            at_south,
        )
        return (back, (kernel_term, bias_term) + terms)

    first_ext, first_saved = forward_block(0, inputs)
    middle = (
        inputs.reshape(-1, channels).astype(jnp.float32) + layer_scale[0] * first_saved[5]
    ).astype(jnp.bfloat16)
    middle = middle.reshape(row_count, col_count, channels)
    second_ext, second_saved = forward_block(1, middle)
    back_second, grads_second = backward_block(1, grad_out, second_saved, second_ext)
    upstream_first = (grad_out.astype(jnp.float32) + back_second).astype(jnp.bfloat16)
    back_first, grads_first = backward_block(0, upstream_first, first_saved, first_ext)
    grad_inputs = (upstream_first.astype(jnp.float32) + back_first).astype(jnp.bfloat16)
    summed = halving_sum(pack_terms(grads_first, grads_second))
    grads_first, grads_second = unpack_terms(summed, grads_first, grads_second)
    inv_root = 1.0 / math.sqrt(cell_total)
    joined = [jnp.stack([grads_first[slot], grads_second[slot]]) * inv_root for slot in range(9)]
    return (
        grad_inputs,
        joined[0],
        joined[1],
        joined[2],
        joined[3],
        joined[4],
        joined[5],
        joined[6],
        joined[7],
        joined[8],
    )


def solution(mesh):
    placed = (
        P("lat", "lon", None),
        P("lat", "lon", None),
        P(),
        P(),
        P(),
        P(),
        P(),
        P(),
        P(),
        P(),
        P(),
    )
    return jax.shard_map(
        per_device,
        mesh=mesh,
        in_specs=placed,
        out_specs=(P("lat", "lon", None), P(), P(), P(), P(), P(), P(), P(), P(), P()),
        check_vma=False,
    )
```

```python
import math

import jax
import jax.numpy as jnp
from jax import lax
from jax.sharding import PartitionSpec as P

EPS = 1e-06
ROOT_TWO_PI = math.sqrt(2.0 / math.pi)
CUBIC = 0.044715


def with_halo(cells, sides, width, closed):
    for axis, dim in sides:
        count = lax.axis_size(axis)
        ends = count if closed else count - 1
        head = lax.slice_in_dim(cells, 0, width, axis=dim)
        tail = lax.slice_in_dim(cells, cells.shape[dim] - width, cells.shape[dim], axis=dim)
        cells = jnp.concatenate(
            [
                lax.ppermute(tail, axis, [(i, (i + 1) % count) for i in range(ends)]),
                cells,
                lax.ppermute(head, axis, [((i + 1) % count, i) for i in range(ends)]),
            ],
            axis=dim,
        )
    return cells


def from_behind(block, axis, distance):
    devices = range(lax.axis_size(axis))
    route = [((i - distance) % len(devices), i) for i in devices]
    return lax.ppermute(block, axis, route)


def gelu_pair(hidden):
    inner = ROOT_TWO_PI * (hidden + CUBIC * hidden * hidden * hidden)
    tanh_val = jnp.tanh(inner)
    value = 0.5 * hidden * (1.0 + tanh_val)
    slope = 0.5 * (1.0 + tanh_val) + 0.5 * hidden * (1.0 - tanh_val * tanh_val) * ROOT_TWO_PI * (
        1.0 + 3.0 * CUBIC * hidden * hidden
    )
    return (value, slope)


def depthwise(extended, kernel, row_count, col_count):
    total = jnp.zeros((row_count, col_count, extended.shape[2]), jnp.float32)
    for tap_row in range(7):
        for tap_col in range(7):
            window = extended[tap_row : tap_row + row_count, tap_col : tap_col + col_count].astype(
                jnp.float32
            )
            total = total + window * kernel[tap_row, tap_col]
    return total


def kernel_grad(grad_cells, extended, row_count, col_count):
    grad_float = grad_cells.astype(jnp.float32)
    rows_out = []
    for tap_row in range(7):
        row_terms = []
        for tap_col in range(7):
            window = extended[tap_row : tap_row + row_count, tap_col : tap_col + col_count].astype(
                jnp.float32
            )
            row_terms.append(jnp.sum(grad_float * window, axis=(0, 1)))
        rows_out.append(jnp.stack(row_terms))
    return jnp.stack(rows_out)


def spread(extended_grad, kernel, row_count, col_count, at_north, at_south):
    row_ids = jnp.arange(row_count + 6)[:, None, None]
    north_mask = jnp.logical_and(at_north, row_ids < 3)
    south_mask = jnp.logical_and(at_south, row_ids >= row_count + 3)
    polar = jnp.logical_or(north_mask, south_mask)
    zeros = jnp.zeros_like(extended_grad)
    normal = jnp.where(polar, zeros, extended_grad)
    north_part = jnp.where(north_mask, extended_grad, zeros)
    south_part = jnp.where(south_mask, extended_grad, zeros)
    result = depthwise(normal, kernel[::-1, ::-1], row_count, col_count)
    upper = depthwise(north_part[0:9], kernel[:, ::-1], 3, col_count)
    lower = depthwise(south_part[row_count - 3 : row_count + 6], kernel[:, ::-1], 3, col_count)
    result = result.at[0:3].add(upper)
    return result.at[row_count - 3 : row_count].add(lower)


def cells_forward(conv_cells, params):
    gain, shift_ln, weight_up, bias_up, weight_down, bias_down, branch_scale = params
    ch_mean = jnp.mean(conv_cells, axis=-1, keepdims=True)
    centred = conv_cells - ch_mean
    ch_var = jnp.mean(centred * centred, axis=-1, keepdims=True)
    inv_std = lax.rsqrt(ch_var + EPS)
    normal_x = centred * inv_std
    normed = (normal_x * gain + shift_ln).astype(jnp.bfloat16)
    hidden = jnp.dot(normed, weight_up, preferred_element_type=jnp.float32) + bias_up
    value, slope = gelu_pair(hidden)
    activ = value.astype(jnp.bfloat16)
    branch = jnp.dot(activ, weight_down, preferred_element_type=jnp.float32) + bias_down
    return (normed, normal_x, inv_std, activ, slope, branch)


def cells_backward(upstream, saved, params):
    normed, normal_x, inv_std, activ, slope, branch = saved
    gain, shift_ln, weight_up, bias_up, weight_down, bias_down, branch_scale = params
    up_float = upstream.astype(jnp.float32)
    d_scale = jnp.sum(up_float * branch, axis=0)
    grad_branch = (up_float * branch_scale).astype(jnp.bfloat16)
    d_bias_down = jnp.sum(grad_branch.astype(jnp.float32), axis=0)
    d_weight_down = jnp.dot(grad_branch.T, activ, preferred_element_type=jnp.float32)
    grad_activ = jnp.dot(grad_branch, weight_down.T, preferred_element_type=jnp.float32)
    grad_hidden = (grad_activ * slope).astype(jnp.bfloat16)
    d_bias_up = jnp.sum(grad_hidden.astype(jnp.float32), axis=0)
    d_weight_up = jnp.dot(normed.T, grad_hidden, preferred_element_type=jnp.float32)
    grad_normed = jnp.dot(grad_hidden, weight_up.T, preferred_element_type=jnp.float32)
    d_gain = jnp.sum(grad_normed * normal_x, axis=0)
    d_shift = jnp.sum(grad_normed, axis=0)
    scaled = grad_normed * gain
    grad_conv = inv_std * (
        scaled
        - jnp.mean(scaled, axis=-1, keepdims=True)
        - normal_x * jnp.mean(scaled * normal_x, axis=-1, keepdims=True)
    )
    return (
        grad_conv.astype(jnp.bfloat16),
        (d_gain, d_shift, d_weight_up, d_bias_up, d_weight_down, d_bias_down, d_scale),
    )


def extend(field, at_north, at_south):
    row_count = field.shape[0]
    lat_ext = with_halo(field, (("lat", 0),), 3, False)
    edge_rows = jnp.where(at_north, field[0:3], field[row_count - 3 : row_count])
    across = from_behind(edge_rows, "lon", lax.axis_size("lon") // 2)[::-1]
    upper = jnp.where(at_north, across, lat_ext[0:3])
    lower = jnp.where(at_south, across, lat_ext[row_count + 3 : row_count + 6])
    stacked = jnp.concatenate([upper, lat_ext[3 : row_count + 3], lower], axis=0)
    return with_halo(stacked, (("lon", 1),), 3, True)


HALVING_ORDER = (("lat", 0), ("lon", 0), ("lon", 1), ("lat", 2), ("lat", 1), ("lon", 2), ("lat", 3), ("lon", 3))


def xor_partners(axis, bit):
    return [(j, j ^ (1 << bit)) for j in range(lax.axis_size(axis))]


def halving_sum(buf, halvings=5):
    steps = []
    for axis, bit in HALVING_ORDER[:halvings]:
        side = (lax.axis_index(axis) >> bit) & 1
        half = buf.shape[0] // 2
        send = lax.dynamic_slice_in_dim(buf, (1 - side) * half, half, axis=0)
        keep = lax.dynamic_slice_in_dim(buf, side * half, half, axis=0)
        buf = keep + lax.ppermute(send, axis, xor_partners(axis, bit))
        steps.append((axis, bit, side))
    for axis, bit in HALVING_ORDER[halvings:]:
        buf = buf + lax.ppermute(buf, axis, xor_partners(axis, bit))
    buf = buf.astype(jnp.bfloat16)
    for axis, bit, side in reversed(steps):
        other = lax.ppermute(buf, axis, xor_partners(axis, bit))
        low = jnp.where(side == 0, buf, other)
        high = jnp.where(side == 0, other, buf)
        buf = jnp.concatenate([low, high], axis=0)
    return buf.astype(jnp.float32)


def pack_terms(grads):
    width = grads[4].shape[1]
    big = jnp.concatenate([grads[4], grads[6]], axis=0)
    flat = jnp.concatenate([piece.reshape(-1) for i, piece in enumerate(grads) if i not in (4, 6)])
    rows = 16
    flat = jnp.pad(flat, (0, rows * width - flat.shape[0]))
    return jnp.concatenate([big, flat.reshape(rows, width)], axis=0)


def unpack_terms(buf, grads):
    size = grads[4].shape[0]
    flat = buf[2 * size :].reshape(-1)
    pieces = []
    offset = 0
    for i, piece in enumerate(grads):
        if i == 4:
            pieces.append(buf[:size])
        elif i == 6:
            pieces.append(buf[size : 2 * size].T)
        else:
            pieces.append(flat[offset : offset + piece.size].reshape(piece.shape))
            offset = offset + piece.size
    return tuple(pieces)


def per_device(
    inputs, grad_out, dw_kernel, dw_bias, ln_gain, ln_bias, w_up, b_up, w_down, b_down, layer_scale
):
    row_count, col_count, channels = inputs.shape
    at_north = lax.axis_index("lat") == 0
    at_south = lax.axis_index("lat") == lax.axis_size("lat") - 1
    cell_total = row_count * lax.axis_size("lat") * col_count * lax.axis_size("lon")

    def params(index):
        return (
            ln_gain[index],
            ln_bias[index],
            w_up[index],
            b_up[index],
            w_down[index],
            b_down[index],
            layer_scale[index],
        )

    def forward_block(index, field):
        extended = extend(field, at_north, at_south)
        conv_out = depthwise(extended, dw_kernel[index], row_count, col_count) + dw_bias[index]
        saved = cells_forward(conv_out.reshape(-1, channels), params(index))
        return (extended, saved)

    def backward_block(index, upstream, saved, extended):
        grad_cells, terms = cells_backward(upstream.reshape(-1, channels), saved, params(index))
        grad_cells = grad_cells.reshape(row_count, col_count, channels)
        kernel_term = kernel_grad(grad_cells, extended, row_count, col_count)
        bias_term = jnp.sum(grad_cells.astype(jnp.float32), axis=(0, 1))
        back = spread(
            extend(grad_cells, at_north, at_south),
            dw_kernel[index],
            row_count,
            col_count,
            at_north,
            at_south,
        )
        return (back, (kernel_term, bias_term) + terms)

    first_ext, first_saved = forward_block(0, inputs)
    middle = (
        inputs.reshape(-1, channels).astype(jnp.float32) + layer_scale[0] * first_saved[5]
    ).astype(jnp.bfloat16)
    middle = middle.reshape(row_count, col_count, channels)
    second_ext, second_saved = forward_block(1, middle)
    back_second, grads_second = backward_block(1, grad_out, second_saved, second_ext)
    grads_second = unpack_terms(halving_sum(pack_terms(grads_second), 4), grads_second)
    upstream_first = (grad_out.astype(jnp.float32) + back_second).astype(jnp.bfloat16)
    back_first, grads_first = backward_block(0, upstream_first, first_saved, first_ext)
    grad_inputs = (upstream_first.astype(jnp.float32) + back_first).astype(jnp.bfloat16)
    grads_first = unpack_terms(halving_sum(pack_terms(grads_first), 4), grads_first)
    inv_root = 1.0 / math.sqrt(cell_total)
    joined = [jnp.stack([grads_first[slot], grads_second[slot]]) * inv_root for slot in range(9)]
    return (
        grad_inputs,
        joined[0],
        joined[1],
        joined[2],
        joined[3],
        joined[4],
        joined[5],
        joined[6],
        joined[7],
        joined[8],
    )


def solution(mesh):
    placed = (
        P("lat", "lon", None),
        P("lat", "lon", None),
        P(),
        P(),
        P(),
        P(),
        P(),
        P(),
        P(),
        P(),
        P(),
    )
    return jax.shard_map(
        per_device,
        mesh=mesh,
        in_specs=placed,
        out_specs=(P("lat", "lon", None), P(), P(), P(), P(), P(), P(), P(), P(), P()),
        check_vma=False,
    )
```

```python
import math

import jax
import jax.numpy as jnp
from jax import lax
from jax.sharding import PartitionSpec as P

EPS = 1e-06
ROOT_TWO_PI = math.sqrt(2.0 / math.pi)
CUBIC = 0.044715


def with_halo(cells, sides, width, closed):
    for axis, dim in sides:
        count = lax.axis_size(axis)
        ends = count if closed else count - 1
        head = lax.slice_in_dim(cells, 0, width, axis=dim)
        tail = lax.slice_in_dim(cells, cells.shape[dim] - width, cells.shape[dim], axis=dim)
        cells = jnp.concatenate(
            [
                lax.ppermute(tail, axis, [(i, (i + 1) % count) for i in range(ends)]),
                cells,
                lax.ppermute(head, axis, [((i + 1) % count, i) for i in range(ends)]),
            ],
            axis=dim,
        )
    return cells


def from_behind(block, axis, distance):
    devices = range(lax.axis_size(axis))
    route = [((i - distance) % len(devices), i) for i in devices]
    return lax.ppermute(block, axis, route)


def gelu_pair(hidden):
    inner = ROOT_TWO_PI * (hidden + CUBIC * hidden * hidden * hidden)
    tanh_val = jnp.tanh(inner)
    value = 0.5 * hidden * (1.0 + tanh_val)
    slope = 0.5 * (1.0 + tanh_val) + 0.5 * hidden * (1.0 - tanh_val * tanh_val) * ROOT_TWO_PI * (
        1.0 + 3.0 * CUBIC * hidden * hidden
    )
    return (value, slope)


def depthwise(extended, kernel, row_count, col_count):
    total = jnp.zeros((row_count, col_count, extended.shape[2]), jnp.float32)
    for tap_row in range(7):
        for tap_col in range(7):
            window = extended[tap_row : tap_row + row_count, tap_col : tap_col + col_count].astype(
                jnp.float32
            )
            total = total + window * kernel[tap_row, tap_col]
    return total


def kernel_grad(grad_cells, extended, row_count, col_count):
    grad_float = grad_cells.astype(jnp.float32)
    rows_out = []
    for tap_row in range(7):
        row_terms = []
        for tap_col in range(7):
            window = extended[tap_row : tap_row + row_count, tap_col : tap_col + col_count].astype(
                jnp.float32
            )
            row_terms.append(jnp.sum(grad_float * window, axis=(0, 1)))
        rows_out.append(jnp.stack(row_terms))
    return jnp.stack(rows_out)


def spread(extended_grad, kernel, row_count, col_count, at_north, at_south):
    row_ids = jnp.arange(row_count + 6)[:, None, None]
    north_mask = jnp.logical_and(at_north, row_ids < 3)
    south_mask = jnp.logical_and(at_south, row_ids >= row_count + 3)
    polar = jnp.logical_or(north_mask, south_mask)
    zeros = jnp.zeros_like(extended_grad)
    normal = jnp.where(polar, zeros, extended_grad)
    north_part = jnp.where(north_mask, extended_grad, zeros)
    south_part = jnp.where(south_mask, extended_grad, zeros)
    result = depthwise(normal, kernel[::-1, ::-1], row_count, col_count)
    upper = depthwise(north_part[0:9], kernel[:, ::-1], 3, col_count)
    lower = depthwise(south_part[row_count - 3 : row_count + 6], kernel[:, ::-1], 3, col_count)
    result = result.at[0:3].add(upper)
    return result.at[row_count - 3 : row_count].add(lower)


def cells_forward(conv_cells, params):
    gain, shift_ln, weight_up, bias_up, weight_down, bias_down, branch_scale = params
    ch_mean = jnp.mean(conv_cells, axis=-1, keepdims=True)
    centred = conv_cells - ch_mean
    ch_var = jnp.mean(centred * centred, axis=-1, keepdims=True)
    inv_std = lax.rsqrt(ch_var + EPS)
    normal_x = centred * inv_std
    normed = (normal_x * gain + shift_ln).astype(jnp.bfloat16)
    hidden = jnp.dot(normed, weight_up, preferred_element_type=jnp.float32) + bias_up
    value, slope = gelu_pair(hidden)
    activ = value.astype(jnp.bfloat16)
    branch = jnp.dot(activ, weight_down, preferred_element_type=jnp.float32) + bias_down
    return (normed, normal_x, inv_std, activ, slope, branch)


def cells_backward(upstream, saved, params):
    normed, normal_x, inv_std, activ, slope, branch = saved
    gain, shift_ln, weight_up, bias_up, weight_down, bias_down, branch_scale = params
    up_float = upstream.astype(jnp.float32)
    d_scale = jnp.sum(up_float * branch, axis=0)
    grad_branch = (up_float * branch_scale).astype(jnp.bfloat16)
    d_bias_down = jnp.sum(grad_branch.astype(jnp.float32), axis=0)
    d_weight_down = jnp.dot(grad_branch.T, activ, preferred_element_type=jnp.float32)
    grad_activ = jnp.dot(grad_branch, weight_down.T, preferred_element_type=jnp.float32)
    grad_hidden = (grad_activ * slope).astype(jnp.bfloat16)
    d_bias_up = jnp.sum(grad_hidden.astype(jnp.float32), axis=0)
    d_weight_up = jnp.dot(normed.T, grad_hidden, preferred_element_type=jnp.float32)
    grad_normed = jnp.dot(grad_hidden, weight_up.T, preferred_element_type=jnp.float32)
    d_gain = jnp.sum(grad_normed * normal_x, axis=0)
    d_shift = jnp.sum(grad_normed, axis=0)
    scaled = grad_normed * gain
    grad_conv = inv_std * (
        scaled
        - jnp.mean(scaled, axis=-1, keepdims=True)
        - normal_x * jnp.mean(scaled * normal_x, axis=-1, keepdims=True)
    )
    return (
        grad_conv.astype(jnp.bfloat16),
        (d_gain, d_shift, d_weight_up, d_bias_up, d_weight_down, d_bias_down, d_scale),
    )


def extend(field, at_north, at_south):
    row_count = field.shape[0]
    lat_ext = with_halo(field, (("lat", 0),), 3, False)
    edge_rows = jnp.where(at_north, field[0:3], field[row_count - 3 : row_count])
    across = from_behind(edge_rows, "lon", lax.axis_size("lon") // 2)[::-1]
    upper = jnp.where(at_north, across, lat_ext[0:3])
    lower = jnp.where(at_south, across, lat_ext[row_count + 3 : row_count + 6])
    stacked = jnp.concatenate([upper, lat_ext[3 : row_count + 3], lower], axis=0)
    return with_halo(stacked, (("lon", 1),), 3, True)


CHAIN_ORDERS = (
    (("lat", 0), ("lon", 0), ("lon", 1), ("lat", 2), ("lat", 1), ("lon", 2), ("lat", 3), ("lon", 3)),
    (("lat", 0), ("lon", 1), ("lat", 2), ("lon", 0), ("lon", 2), ("lat", 1), ("lon", 3), ("lat", 3)),
)


def xor_partners(axis, bit):
    return [(j, j ^ (1 << bit)) for j in range(lax.axis_size(axis))]


def halving_sum(buf, order, halvings):
    steps = []
    for axis, bit in order[:halvings]:
        side = (lax.axis_index(axis) >> bit) & 1
        half = buf.shape[0] // 2
        send = lax.dynamic_slice_in_dim(buf, (1 - side) * half, half, axis=0)
        keep = lax.dynamic_slice_in_dim(buf, side * half, half, axis=0)
        buf = keep + lax.ppermute(send, axis, xor_partners(axis, bit))
        steps.append((axis, bit, side))
    for axis, bit in order[halvings:]:
        buf = buf + lax.ppermute(buf, axis, xor_partners(axis, bit))
    buf = buf.astype(jnp.bfloat16)
    for axis, bit, side in reversed(steps):
        other = lax.ppermute(buf, axis, xor_partners(axis, bit))
        low = jnp.where(side == 0, buf, other)
        high = jnp.where(side == 0, other, buf)
        buf = jnp.concatenate([low, high], axis=0)
    return buf.astype(jnp.float32)


def pack_terms(first, second):
    width = first[4].shape[1]
    big = jnp.concatenate([first[4], second[4], first[6], second[6]], axis=0)
    small = [piece.reshape(-1) for grads in (first, second) for i, piece in enumerate(grads) if i not in (4, 6)]
    flat = jnp.concatenate(small)
    rows = 32
    flat = jnp.pad(flat, (0, rows * width - flat.shape[0]))
    return jnp.concatenate([big, flat.reshape(rows, width)], axis=0)


def unpack_terms(buf, first, second):
    size = first[4].shape[0]
    big = buf[: 4 * size]
    flat = buf[4 * size :].reshape(-1)
    out = []
    offset = 0
    for b, grads in enumerate((first, second)):
        pieces = []
        for i, piece in enumerate(grads):
            if i == 4:
                pieces.append(big[b * size : (b + 1) * size])
            elif i == 6:
                pieces.append(big[(2 + b) * size : (3 + b) * size].T)
            else:
                pieces.append(flat[offset : offset + piece.size].reshape(piece.shape))
                offset = offset + piece.size
        out.append(tuple(pieces))
    return out


def per_device(
    inputs, grad_out, dw_kernel, dw_bias, ln_gain, ln_bias, w_up, b_up, w_down, b_down, layer_scale
):
    row_count, col_count, channels = inputs.shape
    at_north = lax.axis_index("lat") == 0
    at_south = lax.axis_index("lat") == lax.axis_size("lat") - 1
    cell_total = row_count * lax.axis_size("lat") * col_count * lax.axis_size("lon")

    def params(index):
        return (
            ln_gain[index],
            ln_bias[index],
            w_up[index],
            b_up[index],
            w_down[index],
            b_down[index],
            layer_scale[index],
        )

    def forward_block(index, field):
        extended = extend(field, at_north, at_south)
        conv_out = depthwise(extended, dw_kernel[index], row_count, col_count) + dw_bias[index]
        saved = cells_forward(conv_out.reshape(-1, channels), params(index))
        return (extended, saved)

    def backward_block(index, upstream, saved, extended):
        grad_cells, terms = cells_backward(upstream.reshape(-1, channels), saved, params(index))
        grad_cells = grad_cells.reshape(row_count, col_count, channels)
        kernel_term = kernel_grad(grad_cells, extended, row_count, col_count)
        bias_term = jnp.sum(grad_cells.astype(jnp.float32), axis=(0, 1))
        back = spread(
            extend(grad_cells, at_north, at_south),
            dw_kernel[index],
            row_count,
            col_count,
            at_north,
            at_south,
        )
        return (back, (kernel_term, bias_term) + terms)

    first_ext, first_saved = forward_block(0, inputs)
    middle = (
        inputs.reshape(-1, channels).astype(jnp.float32) + layer_scale[0] * first_saved[5]
    ).astype(jnp.bfloat16)
    middle = middle.reshape(row_count, col_count, channels)
    second_ext, second_saved = forward_block(1, middle)
    back_second, grads_second = backward_block(1, grad_out, second_saved, second_ext)
    upstream_first = (grad_out.astype(jnp.float32) + back_second).astype(jnp.bfloat16)
    back_first, grads_first = backward_block(0, upstream_first, first_saved, first_ext)
    grad_inputs = (upstream_first.astype(jnp.float32) + back_first).astype(jnp.bfloat16)
    packed = pack_terms(grads_first, grads_second)
    rows = packed.shape[0] // len(CHAIN_ORDERS)
    summed = jnp.concatenate(
        [
            halving_sum(packed[c * rows : (c + 1) * rows], order, 4)
            for c, order in enumerate(CHAIN_ORDERS)
        ],
        axis=0,
    )
    grads_first, grads_second = unpack_terms(summed, grads_first, grads_second)
    inv_root = 1.0 / math.sqrt(cell_total)
    joined = [jnp.stack([grads_first[slot], grads_second[slot]]) * inv_root for slot in range(9)]
    return (
        grad_inputs,
        joined[0],
        joined[1],
        joined[2],
        joined[3],
        joined[4],
        joined[5],
        joined[6],
        joined[7],
        joined[8],
    )


def solution(mesh):
    placed = (
        P("lat", "lon", None),
        P("lat", "lon", None),
        P(),
        P(),
        P(),
        P(),
        P(),
        P(),
        P(),
        P(),
        P(),
    )
    return jax.shard_map(
        per_device,
        mesh=mesh,
        in_specs=placed,
        out_specs=(P("lat", "lon", None), P(), P(), P(), P(), P(), P(), P(), P(), P()),
        check_vma=False,
    )
```

```python
import math

import jax
import jax.numpy as jnp
from jax import lax
from jax.sharding import PartitionSpec as P

EPS = 1e-06
ROOT_TWO_PI = math.sqrt(2.0 / math.pi)
CUBIC = 0.044715


def with_halo(cells, sides, width, closed):
    for axis, dim in sides:
        count = lax.axis_size(axis)
        ends = count if closed else count - 1
        head = lax.slice_in_dim(cells, 0, width, axis=dim)
        tail = lax.slice_in_dim(cells, cells.shape[dim] - width, cells.shape[dim], axis=dim)
        cells = jnp.concatenate(
            [
                lax.ppermute(tail, axis, [(i, (i + 1) % count) for i in range(ends)]),
                cells,
                lax.ppermute(head, axis, [((i + 1) % count, i) for i in range(ends)]),
            ],
            axis=dim,
        )
    return cells


def from_behind(block, axis, distance):
    devices = range(lax.axis_size(axis))
    route = [((i - distance) % len(devices), i) for i in devices]
    return lax.ppermute(block, axis, route)


def gelu_pair(hidden):
    inner = ROOT_TWO_PI * (hidden + CUBIC * hidden * hidden * hidden)
    tanh_val = jnp.tanh(inner)
    value = 0.5 * hidden * (1.0 + tanh_val)
    slope = 0.5 * (1.0 + tanh_val) + 0.5 * hidden * (1.0 - tanh_val * tanh_val) * ROOT_TWO_PI * (
        1.0 + 3.0 * CUBIC * hidden * hidden
    )
    return (value, slope)


def depthwise(extended, kernel, row_count, col_count):
    total = jnp.zeros((row_count, col_count, extended.shape[2]), jnp.float32)
    for tap_row in range(7):
        for tap_col in range(7):
            window = extended[tap_row : tap_row + row_count, tap_col : tap_col + col_count].astype(
                jnp.float32
            )
            total = total + window * kernel[tap_row, tap_col]
    return total


def kernel_grad(grad_cells, extended, row_count, col_count):
    grad_float = grad_cells.astype(jnp.float32)
    rows_out = []
    for tap_row in range(7):
        row_terms = []
        for tap_col in range(7):
            window = extended[tap_row : tap_row + row_count, tap_col : tap_col + col_count].astype(
                jnp.float32
            )
            row_terms.append(jnp.sum(grad_float * window, axis=(0, 1)))
        rows_out.append(jnp.stack(row_terms))
    return jnp.stack(rows_out)


def spread(extended_grad, kernel, row_count, col_count, at_north, at_south):
    row_ids = jnp.arange(row_count + 6)[:, None, None]
    north_mask = jnp.logical_and(at_north, row_ids < 3)
    south_mask = jnp.logical_and(at_south, row_ids >= row_count + 3)
    polar = jnp.logical_or(north_mask, south_mask)
    zeros = jnp.zeros_like(extended_grad)
    normal = jnp.where(polar, zeros, extended_grad)
    north_part = jnp.where(north_mask, extended_grad, zeros)
    south_part = jnp.where(south_mask, extended_grad, zeros)
    result = depthwise(normal, kernel[::-1, ::-1], row_count, col_count)
    upper = depthwise(north_part[0:9], kernel[:, ::-1], 3, col_count)
    lower = depthwise(south_part[row_count - 3 : row_count + 6], kernel[:, ::-1], 3, col_count)
    result = result.at[0:3].add(upper)
    return result.at[row_count - 3 : row_count].add(lower)


def cells_forward(conv_cells, params):
    gain, shift_ln, weight_up, bias_up, weight_down, bias_down, branch_scale = params
    ch_mean = jnp.mean(conv_cells, axis=-1, keepdims=True)
    centred = conv_cells - ch_mean
    ch_var = jnp.mean(centred * centred, axis=-1, keepdims=True)
    inv_std = lax.rsqrt(ch_var + EPS)
    normal_x = centred * inv_std
    normed = (normal_x * gain + shift_ln).astype(jnp.bfloat16)
    hidden = jnp.dot(normed, weight_up, preferred_element_type=jnp.float32) + bias_up
    value, slope = gelu_pair(hidden)
    activ = value.astype(jnp.bfloat16)
    branch = jnp.dot(activ, weight_down, preferred_element_type=jnp.float32) + bias_down
    return (normed, normal_x, inv_std, activ, slope, branch)


def cells_backward(upstream, saved, params):
    normed, normal_x, inv_std, activ, slope, branch = saved
    gain, shift_ln, weight_up, bias_up, weight_down, bias_down, branch_scale = params
    up_float = upstream.astype(jnp.float32)
    d_scale = jnp.sum(up_float * branch, axis=0)
    grad_branch = (up_float * branch_scale).astype(jnp.bfloat16)
    d_bias_down = jnp.sum(grad_branch.astype(jnp.float32), axis=0)
    d_weight_down = jnp.dot(grad_branch.T, activ, preferred_element_type=jnp.float32)
    grad_activ = jnp.dot(grad_branch, weight_down.T, preferred_element_type=jnp.float32)
    grad_hidden = (grad_activ * slope).astype(jnp.bfloat16)
    d_bias_up = jnp.sum(grad_hidden.astype(jnp.float32), axis=0)
    d_weight_up = jnp.dot(normed.T, grad_hidden, preferred_element_type=jnp.float32)
    grad_normed = jnp.dot(grad_hidden, weight_up.T, preferred_element_type=jnp.float32)
    d_gain = jnp.sum(grad_normed * normal_x, axis=0)
    d_shift = jnp.sum(grad_normed, axis=0)
    scaled = grad_normed * gain
    grad_conv = inv_std * (
        scaled
        - jnp.mean(scaled, axis=-1, keepdims=True)
        - normal_x * jnp.mean(scaled * normal_x, axis=-1, keepdims=True)
    )
    return (
        grad_conv.astype(jnp.bfloat16),
        (d_gain, d_shift, d_weight_up, d_bias_up, d_weight_down, d_bias_down, d_scale),
    )


def extend(field, at_north, at_south):
    row_count = field.shape[0]
    lat_ext = with_halo(field, (("lat", 0),), 3, False)
    edge_rows = jnp.where(at_north, field[0:3], field[row_count - 3 : row_count])
    across = from_behind(edge_rows, "lon", lax.axis_size("lon") // 2)[::-1]
    upper = jnp.where(at_north, across, lat_ext[0:3])
    lower = jnp.where(at_south, across, lat_ext[row_count + 3 : row_count + 6])
    stacked = jnp.concatenate([upper, lat_ext[3 : row_count + 3], lower], axis=0)
    return with_halo(stacked, (("lon", 1),), 3, True)


CHAIN_ORDERS = (
    (("lat", 0), ("lon", 0), ("lon", 1), ("lat", 2), ("lat", 1), ("lon", 2), ("lat", 3), ("lon", 3)),
    (("lat", 0), ("lon", 1), ("lat", 2), ("lon", 0), ("lon", 2), ("lat", 1), ("lon", 3), ("lat", 3)),
)


def xor_partners(axis, bit):
    return [(j, j ^ (1 << bit)) for j in range(lax.axis_size(axis))]


def halving_sum(buf, order, halvings, hook=None):
    steps = []
    for axis, bit in order[:halvings]:
        side = (lax.axis_index(axis) >> bit) & 1
        half = buf.shape[0] // 2
        send = lax.dynamic_slice_in_dim(buf, (1 - side) * half, half, axis=0)
        keep = lax.dynamic_slice_in_dim(buf, side * half, half, axis=0)
        buf = keep + lax.ppermute(send, axis, xor_partners(axis, bit))
        if hook is not None and not steps:
            buf = hook(buf)
        steps.append((axis, bit, side))
    for axis, bit in order[halvings:]:
        buf = buf + lax.ppermute(buf, axis, xor_partners(axis, bit))
    buf = buf.astype(jnp.bfloat16)
    for axis, bit, side in reversed(steps):
        other = lax.ppermute(buf, axis, xor_partners(axis, bit))
        low = jnp.where(side == 0, buf, other)
        high = jnp.where(side == 0, other, buf)
        buf = jnp.concatenate([low, high], axis=0)
    return buf.astype(jnp.float32)


def pack_terms(first, second):
    width = first[4].shape[1]
    big = jnp.concatenate([first[4], second[4], first[6], second[6]], axis=0)
    small = [piece.reshape(-1) for grads in (first, second) for i, piece in enumerate(grads) if i not in (4, 6)]
    flat = jnp.concatenate(small)
    rows = 32
    flat = jnp.pad(flat, (0, rows * width - flat.shape[0]))
    return jnp.concatenate([big, flat.reshape(rows, width)], axis=0)


def unpack_terms(buf, first, second):
    size = first[4].shape[0]
    big = buf[: 4 * size]
    flat = buf[4 * size :].reshape(-1)
    out = []
    offset = 0
    for b, grads in enumerate((first, second)):
        pieces = []
        for i, piece in enumerate(grads):
            if i == 4:
                pieces.append(big[b * size : (b + 1) * size])
            elif i == 6:
                pieces.append(big[(2 + b) * size : (3 + b) * size].T)
            else:
                pieces.append(flat[offset : offset + piece.size].reshape(piece.shape))
                offset = offset + piece.size
        out.append(tuple(pieces))
    return out


def per_device(
    inputs, grad_out, dw_kernel, dw_bias, ln_gain, ln_bias, w_up, b_up, w_down, b_down, layer_scale
):
    row_count, col_count, channels = inputs.shape
    at_north = lax.axis_index("lat") == 0
    at_south = lax.axis_index("lat") == lax.axis_size("lat") - 1
    cell_total = row_count * lax.axis_size("lat") * col_count * lax.axis_size("lon")

    def params(index):
        return (
            ln_gain[index],
            ln_bias[index],
            w_up[index],
            b_up[index],
            w_down[index],
            b_down[index],
            layer_scale[index],
        )

    def forward_block(index, field):
        extended = extend(field, at_north, at_south)
        conv_out = depthwise(extended, dw_kernel[index], row_count, col_count) + dw_bias[index]
        saved = cells_forward(conv_out.reshape(-1, channels), params(index))
        return (extended, saved)

    def backward_cells(index, upstream, saved, extended):
        grad_cells, terms = cells_backward(upstream.reshape(-1, channels), saved, params(index))
        grad_cells = grad_cells.reshape(row_count, col_count, channels)
        kernel_term = kernel_grad(grad_cells, extended, row_count, col_count)
        bias_term = jnp.sum(grad_cells.astype(jnp.float32), axis=(0, 1))
        return grad_cells, (kernel_term, bias_term) + terms

    def backward_block(index, upstream, saved, extended):
        grad_cells, terms = backward_cells(index, upstream, saved, extended)
        back = spread(
            extend(grad_cells, at_north, at_south),
            dw_kernel[index],
            row_count,
            col_count,
            at_north,
            at_south,
        )
        return (back, terms)

    first_ext, first_saved = forward_block(0, inputs)
    middle = (
        inputs.reshape(-1, channels).astype(jnp.float32) + layer_scale[0] * first_saved[5]
    ).astype(jnp.bfloat16)
    middle = middle.reshape(row_count, col_count, channels)
    second_ext, second_saved = forward_block(1, middle)
    back_second, grads_second = backward_block(1, grad_out, second_saved, second_ext)
    upstream_first = (grad_out.astype(jnp.float32) + back_second).astype(jnp.bfloat16)
    grad_cells_first, grads_first = backward_cells(0, upstream_first, first_saved, first_ext)
    pending = {}

    def start_back(buf):
        buf, cells = lax.optimization_barrier((buf, grad_cells_first))
        pending["back"] = spread(
            extend(cells, at_north, at_south), dw_kernel[0], row_count, col_count, at_north, at_south
        )
        return buf

    packed = pack_terms(grads_first, grads_second)
    rows = packed.shape[0] // len(CHAIN_ORDERS)
    summed = jnp.concatenate(
        [
            halving_sum(packed[c * rows : (c + 1) * rows], order, 4, start_back if c == 0 else None)
            for c, order in enumerate(CHAIN_ORDERS)
        ],
        axis=0,
    )
    grads_first, grads_second = unpack_terms(summed, grads_first, grads_second)
    grad_inputs = (upstream_first.astype(jnp.float32) + pending["back"]).astype(jnp.bfloat16)
    inv_root = 1.0 / math.sqrt(cell_total)
    joined = [jnp.stack([grads_first[slot], grads_second[slot]]) * inv_root for slot in range(9)]
    return (
        grad_inputs,
        joined[0],
        joined[1],
        joined[2],
        joined[3],
        joined[4],
        joined[5],
        joined[6],
        joined[7],
        joined[8],
    )


def solution(mesh):
    placed = (
        P("lat", "lon", None),
        P("lat", "lon", None),
        P(),
        P(),
        P(),
        P(),
        P(),
        P(),
        P(),
        P(),
        P(),
    )
    return jax.shard_map(
        per_device,
        mesh=mesh,
        in_specs=placed,
        out_specs=(P("lat", "lon", None), P(), P(), P(), P(), P(), P(), P(), P(), P()),
        check_vma=False,
    )
```

```python
import math

import jax
import jax.numpy as jnp
from jax import lax
from jax.sharding import PartitionSpec as P

EPS = 1e-06
ROOT_TWO_PI = math.sqrt(2.0 / math.pi)
CUBIC = 0.044715


def with_halo(cells, sides, width, closed):
    for axis, dim in sides:
        count = lax.axis_size(axis)
        ends = count if closed else count - 1
        head = lax.slice_in_dim(cells, 0, width, axis=dim)
        tail = lax.slice_in_dim(cells, cells.shape[dim] - width, cells.shape[dim], axis=dim)
        cells = jnp.concatenate(
            [
                lax.ppermute(tail, axis, [(i, (i + 1) % count) for i in range(ends)]),
                cells,
                lax.ppermute(head, axis, [((i + 1) % count, i) for i in range(ends)]),
            ],
            axis=dim,
        )
    return cells


def from_behind(block, axis, distance):
    devices = range(lax.axis_size(axis))
    route = [((i - distance) % len(devices), i) for i in devices]
    return lax.ppermute(block, axis, route)


def gelu_pair(hidden):
    inner = ROOT_TWO_PI * (hidden + CUBIC * hidden * hidden * hidden)
    tanh_val = jnp.tanh(inner)
    value = 0.5 * hidden * (1.0 + tanh_val)
    slope = 0.5 * (1.0 + tanh_val) + 0.5 * hidden * (1.0 - tanh_val * tanh_val) * ROOT_TWO_PI * (
        1.0 + 3.0 * CUBIC * hidden * hidden
    )
    return (value, slope)


def depthwise(extended, kernel, row_count, col_count):
    total = jnp.zeros((row_count, col_count, extended.shape[2]), jnp.float32)
    for tap_row in range(7):
        for tap_col in range(7):
            window = extended[tap_row : tap_row + row_count, tap_col : tap_col + col_count].astype(
                jnp.float32
            )
            total = total + window * kernel[tap_row, tap_col]
    return total


def kernel_grad(grad_cells, extended, row_count, col_count):
    grad_float = grad_cells.astype(jnp.float32)
    rows_out = []
    for tap_row in range(7):
        row_terms = []
        for tap_col in range(7):
            window = extended[tap_row : tap_row + row_count, tap_col : tap_col + col_count].astype(
                jnp.float32
            )
            row_terms.append(jnp.sum(grad_float * window, axis=(0, 1)))
        rows_out.append(jnp.stack(row_terms))
    return jnp.stack(rows_out)


def spread(extended_grad, kernel, row_count, col_count, at_north, at_south):
    row_ids = jnp.arange(row_count + 6)[:, None, None]
    north_mask = jnp.logical_and(at_north, row_ids < 3)
    south_mask = jnp.logical_and(at_south, row_ids >= row_count + 3)
    polar = jnp.logical_or(north_mask, south_mask)
    zeros = jnp.zeros_like(extended_grad)
    normal = jnp.where(polar, zeros, extended_grad)
    north_part = jnp.where(north_mask, extended_grad, zeros)
    south_part = jnp.where(south_mask, extended_grad, zeros)
    result = depthwise(normal, kernel[::-1, ::-1], row_count, col_count)
    upper = depthwise(north_part[0:9], kernel[:, ::-1], 3, col_count)
    lower = depthwise(south_part[row_count - 3 : row_count + 6], kernel[:, ::-1], 3, col_count)
    result = result.at[0:3].add(upper)
    return result.at[row_count - 3 : row_count].add(lower)


def cells_forward(conv_cells, params):
    gain, shift_ln, weight_up, bias_up, weight_down, bias_down, branch_scale = params
    ch_mean = jnp.mean(conv_cells, axis=-1, keepdims=True)
    centred = conv_cells - ch_mean
    ch_var = jnp.mean(centred * centred, axis=-1, keepdims=True)
    inv_std = lax.rsqrt(ch_var + EPS)
    normal_x = centred * inv_std
    normed = (normal_x * gain + shift_ln).astype(jnp.bfloat16)
    hidden = jnp.dot(normed, weight_up, preferred_element_type=jnp.float32) + bias_up
    value, slope = gelu_pair(hidden)
    activ = value.astype(jnp.bfloat16)
    branch = jnp.dot(activ, weight_down, preferred_element_type=jnp.float32) + bias_down
    return (normed, normal_x, inv_std, activ, slope, branch)


def cells_backward(upstream, saved, params):
    normed, normal_x, inv_std, activ, slope, branch = saved
    gain, shift_ln, weight_up, bias_up, weight_down, bias_down, branch_scale = params
    up_float = upstream.astype(jnp.float32)
    d_scale = jnp.sum(up_float * branch, axis=0)
    grad_branch = (up_float * branch_scale).astype(jnp.bfloat16)
    d_bias_down = jnp.sum(grad_branch.astype(jnp.float32), axis=0)
    d_weight_down = jnp.dot(grad_branch.T, activ, preferred_element_type=jnp.float32)
    grad_activ = jnp.dot(grad_branch, weight_down.T, preferred_element_type=jnp.float32)
    grad_hidden = (grad_activ * slope).astype(jnp.bfloat16)
    d_bias_up = jnp.sum(grad_hidden.astype(jnp.float32), axis=0)
    d_weight_up = jnp.dot(normed.T, grad_hidden, preferred_element_type=jnp.float32)
    grad_normed = jnp.dot(grad_hidden, weight_up.T, preferred_element_type=jnp.float32)
    d_gain = jnp.sum(grad_normed * normal_x, axis=0)
    d_shift = jnp.sum(grad_normed, axis=0)
    scaled = grad_normed * gain
    grad_conv = inv_std * (
        scaled
        - jnp.mean(scaled, axis=-1, keepdims=True)
        - normal_x * jnp.mean(scaled * normal_x, axis=-1, keepdims=True)
    )
    return (
        grad_conv.astype(jnp.bfloat16),
        (d_gain, d_shift, d_weight_up, d_bias_up, d_weight_down, d_bias_down, d_scale),
    )


def extend(field, at_north, at_south):
    row_count = field.shape[0]
    lat_ext = with_halo(field, (("lat", 0),), 3, False)
    edge_rows = jnp.where(at_north, field[0:3], field[row_count - 3 : row_count])
    across = from_behind(edge_rows, "lon", lax.axis_size("lon") // 2)[::-1]
    upper = jnp.where(at_north, across, lat_ext[0:3])
    lower = jnp.where(at_south, across, lat_ext[row_count + 3 : row_count + 6])
    stacked = jnp.concatenate([upper, lat_ext[3 : row_count + 3], lower], axis=0)
    return with_halo(stacked, (("lon", 1),), 3, True)


CHAIN_ORDERS = (
    (("lat", 0), ("lon", 0), ("lon", 1), ("lat", 2), ("lat", 1), ("lon", 2), ("lat", 3), ("lon", 3)),
    (("lat", 0), ("lon", 1), ("lat", 2), ("lon", 0), ("lon", 2), ("lat", 1), ("lon", 3), ("lat", 3)),
)


def xor_partners(axis, bit):
    return [(j, j ^ (1 << bit)) for j in range(lax.axis_size(axis))]


def halving_sum(buf, order, halvings, hook=None):
    steps = []
    for axis, bit in order[:halvings]:
        side = (lax.axis_index(axis) >> bit) & 1
        half = buf.shape[0] // 2
        send = lax.dynamic_slice_in_dim(buf, (1 - side) * half, half, axis=0)
        keep = lax.dynamic_slice_in_dim(buf, side * half, half, axis=0)
        buf = keep + lax.ppermute(send, axis, xor_partners(axis, bit))
        if hook is not None and len(steps) == halvings - 1:
            buf = hook(buf)
        steps.append((axis, bit, side))
    for axis, bit in order[halvings:]:
        buf = buf + lax.ppermute(buf, axis, xor_partners(axis, bit))
    buf = buf.astype(jnp.bfloat16)
    for axis, bit, side in reversed(steps):
        other = lax.ppermute(buf, axis, xor_partners(axis, bit))
        low = jnp.where(side == 0, buf, other)
        high = jnp.where(side == 0, other, buf)
        buf = jnp.concatenate([low, high], axis=0)
    return buf.astype(jnp.float32)


def pack_terms(first, second):
    width = first[4].shape[1]
    big = jnp.concatenate([first[4], second[4], first[6], second[6]], axis=0)
    small = [piece.reshape(-1) for grads in (first, second) for i, piece in enumerate(grads) if i not in (4, 6)]
    flat = jnp.concatenate(small)
    rows = 32
    flat = jnp.pad(flat, (0, rows * width - flat.shape[0]))
    return jnp.concatenate([big, flat.reshape(rows, width)], axis=0)


def unpack_terms(buf, first, second):
    size = first[4].shape[0]
    big = buf[: 4 * size]
    flat = buf[4 * size :].reshape(-1)
    out = []
    offset = 0
    for b, grads in enumerate((first, second)):
        pieces = []
        for i, piece in enumerate(grads):
            if i == 4:
                pieces.append(big[b * size : (b + 1) * size])
            elif i == 6:
                pieces.append(big[(2 + b) * size : (3 + b) * size].T)
            else:
                pieces.append(flat[offset : offset + piece.size].reshape(piece.shape))
                offset = offset + piece.size
        out.append(tuple(pieces))
    return out


def per_device(
    inputs, grad_out, dw_kernel, dw_bias, ln_gain, ln_bias, w_up, b_up, w_down, b_down, layer_scale
):
    row_count, col_count, channels = inputs.shape
    at_north = lax.axis_index("lat") == 0
    at_south = lax.axis_index("lat") == lax.axis_size("lat") - 1
    cell_total = row_count * lax.axis_size("lat") * col_count * lax.axis_size("lon")

    def params(index):
        return (
            ln_gain[index],
            ln_bias[index],
            w_up[index],
            b_up[index],
            w_down[index],
            b_down[index],
            layer_scale[index],
        )

    def forward_block(index, field):
        extended = extend(field, at_north, at_south)
        conv_out = depthwise(extended, dw_kernel[index], row_count, col_count) + dw_bias[index]
        saved = cells_forward(conv_out.reshape(-1, channels), params(index))
        return (extended, saved)

    def backward_cells(index, upstream, saved, extended):
        grad_cells, terms = cells_backward(upstream.reshape(-1, channels), saved, params(index))
        grad_cells = grad_cells.reshape(row_count, col_count, channels)
        kernel_term = kernel_grad(grad_cells, extended, row_count, col_count)
        bias_term = jnp.sum(grad_cells.astype(jnp.float32), axis=(0, 1))
        return grad_cells, (kernel_term, bias_term) + terms

    def backward_block(index, upstream, saved, extended):
        grad_cells, terms = backward_cells(index, upstream, saved, extended)
        back = spread(
            extend(grad_cells, at_north, at_south),
            dw_kernel[index],
            row_count,
            col_count,
            at_north,
            at_south,
        )
        return (back, terms)

    first_ext, first_saved = forward_block(0, inputs)
    middle = (
        inputs.reshape(-1, channels).astype(jnp.float32) + layer_scale[0] * first_saved[5]
    ).astype(jnp.bfloat16)
    middle = middle.reshape(row_count, col_count, channels)
    second_ext, second_saved = forward_block(1, middle)
    back_second, grads_second = backward_block(1, grad_out, second_saved, second_ext)
    upstream_first = (grad_out.astype(jnp.float32) + back_second).astype(jnp.bfloat16)
    grad_cells_first, grads_first = backward_cells(0, upstream_first, first_saved, first_ext)
    pending = {}

    def start_back(buf):
        buf, cells = lax.optimization_barrier((buf, grad_cells_first))
        pending["back"] = spread(
            extend(cells, at_north, at_south), dw_kernel[0], row_count, col_count, at_north, at_south
        )
        return buf

    packed = pack_terms(grads_first, grads_second)
    rows = packed.shape[0] // len(CHAIN_ORDERS)
    summed = jnp.concatenate(
        [
            halving_sum(packed[c * rows : (c + 1) * rows], order, 4, start_back if c == 0 else None)
            for c, order in enumerate(CHAIN_ORDERS)
        ],
        axis=0,
    )
    grads_first, grads_second = unpack_terms(summed, grads_first, grads_second)
    grad_inputs = (upstream_first.astype(jnp.float32) + pending["back"]).astype(jnp.bfloat16)
    inv_root = 1.0 / math.sqrt(cell_total)
    joined = [jnp.stack([grads_first[slot], grads_second[slot]]) * inv_root for slot in range(9)]
    return (
        grad_inputs,
        joined[0],
        joined[1],
        joined[2],
        joined[3],
        joined[4],
        joined[5],
        joined[6],
        joined[7],
        joined[8],
    )


def solution(mesh):
    placed = (
        P("lat", "lon", None),
        P("lat", "lon", None),
        P(),
        P(),
        P(),
        P(),
        P(),
        P(),
        P(),
        P(),
        P(),
    )
    return jax.shard_map(
        per_device,
        mesh=mesh,
        in_specs=placed,
        out_specs=(P("lat", "lon", None), P(), P(), P(), P(), P(), P(), P(), P(), P()),
        check_vma=False,
    )
```

```python
import math

import jax
import jax.numpy as jnp
from jax import lax
from jax.sharding import PartitionSpec as P

EPS = 1e-06
ROOT_TWO_PI = math.sqrt(2.0 / math.pi)
CUBIC = 0.044715


def with_halo(cells, sides, width, closed):
    for axis, dim in sides:
        count = lax.axis_size(axis)
        ends = count if closed else count - 1
        head = lax.slice_in_dim(cells, 0, width, axis=dim)
        tail = lax.slice_in_dim(cells, cells.shape[dim] - width, cells.shape[dim], axis=dim)
        cells = jnp.concatenate(
            [
                lax.ppermute(tail, axis, [(i, (i + 1) % count) for i in range(ends)]),
                cells,
                lax.ppermute(head, axis, [((i + 1) % count, i) for i in range(ends)]),
            ],
            axis=dim,
        )
    return cells


def from_behind(block, axis, distance):
    devices = range(lax.axis_size(axis))
    route = [((i - distance) % len(devices), i) for i in devices]
    return lax.ppermute(block, axis, route)


def gelu_pair(hidden):
    inner = ROOT_TWO_PI * (hidden + CUBIC * hidden * hidden * hidden)
    tanh_val = jnp.tanh(inner)
    value = 0.5 * hidden * (1.0 + tanh_val)
    slope = 0.5 * (1.0 + tanh_val) + 0.5 * hidden * (1.0 - tanh_val * tanh_val) * ROOT_TWO_PI * (
        1.0 + 3.0 * CUBIC * hidden * hidden
    )
    return (value, slope)


def depthwise(extended, kernel, row_count, col_count):
    total = jnp.zeros((row_count, col_count, extended.shape[2]), jnp.float32)
    for tap_row in range(7):
        for tap_col in range(7):
            window = extended[tap_row : tap_row + row_count, tap_col : tap_col + col_count].astype(
                jnp.float32
            )
            total = total + window * kernel[tap_row, tap_col]
    return total


def kernel_grad(grad_cells, extended, row_count, col_count):
    grad_float = grad_cells.astype(jnp.float32)
    rows_out = []
    for tap_row in range(7):
        row_terms = []
        for tap_col in range(7):
            window = extended[tap_row : tap_row + row_count, tap_col : tap_col + col_count].astype(
                jnp.float32
            )
            row_terms.append(jnp.sum(grad_float * window, axis=(0, 1)))
        rows_out.append(jnp.stack(row_terms))
    return jnp.stack(rows_out)


def spread(extended_grad, kernel, row_count, col_count, at_north, at_south):
    row_ids = jnp.arange(row_count + 6)[:, None, None]
    north_mask = jnp.logical_and(at_north, row_ids < 3)
    south_mask = jnp.logical_and(at_south, row_ids >= row_count + 3)
    polar = jnp.logical_or(north_mask, south_mask)
    zeros = jnp.zeros_like(extended_grad)
    normal = jnp.where(polar, zeros, extended_grad)
    north_part = jnp.where(north_mask, extended_grad, zeros)
    south_part = jnp.where(south_mask, extended_grad, zeros)
    result = depthwise(normal, kernel[::-1, ::-1], row_count, col_count)
    upper = depthwise(north_part[0:9], kernel[:, ::-1], 3, col_count)
    lower = depthwise(south_part[row_count - 3 : row_count + 6], kernel[:, ::-1], 3, col_count)
    result = result.at[0:3].add(upper)
    return result.at[row_count - 3 : row_count].add(lower)


def cells_forward(conv_cells, params):
    gain, shift_ln, weight_up, bias_up, weight_down, bias_down, branch_scale = params
    ch_mean = jnp.mean(conv_cells, axis=-1, keepdims=True)
    centred = conv_cells - ch_mean
    ch_var = jnp.mean(centred * centred, axis=-1, keepdims=True)
    inv_std = lax.rsqrt(ch_var + EPS)
    normal_x = centred * inv_std
    normed = (normal_x * gain + shift_ln).astype(jnp.bfloat16)
    hidden = jnp.dot(normed, weight_up, preferred_element_type=jnp.float32) + bias_up
    value, slope = gelu_pair(hidden)
    activ = value.astype(jnp.bfloat16)
    branch = jnp.dot(activ, weight_down, preferred_element_type=jnp.float32) + bias_down
    return (normed, normal_x, inv_std, activ, slope, branch)


def cells_backward(upstream, saved, params):
    normed, normal_x, inv_std, activ, slope, branch = saved
    gain, shift_ln, weight_up, bias_up, weight_down, bias_down, branch_scale = params
    up_float = upstream.astype(jnp.float32)
    d_scale = jnp.sum(up_float * branch, axis=0)
    grad_branch = (up_float * branch_scale).astype(jnp.bfloat16)
    d_bias_down = jnp.sum(grad_branch.astype(jnp.float32), axis=0)
    d_weight_down = jnp.dot(grad_branch.T, activ, preferred_element_type=jnp.float32)
    grad_activ = jnp.dot(grad_branch, weight_down.T, preferred_element_type=jnp.float32)
    grad_hidden = (grad_activ * slope).astype(jnp.bfloat16)
    d_bias_up = jnp.sum(grad_hidden.astype(jnp.float32), axis=0)
    d_weight_up = jnp.dot(normed.T, grad_hidden, preferred_element_type=jnp.float32)
    grad_normed = jnp.dot(grad_hidden, weight_up.T, preferred_element_type=jnp.float32)
    d_gain = jnp.sum(grad_normed * normal_x, axis=0)
    d_shift = jnp.sum(grad_normed, axis=0)
    scaled = grad_normed * gain
    grad_conv = inv_std * (
        scaled
        - jnp.mean(scaled, axis=-1, keepdims=True)
        - normal_x * jnp.mean(scaled * normal_x, axis=-1, keepdims=True)
    )
    return (
        grad_conv.astype(jnp.bfloat16),
        (d_gain, d_shift, d_weight_up, d_bias_up, d_weight_down, d_bias_down, d_scale),
    )


def extend(field, at_north, at_south):
    row_count = field.shape[0]
    lat_ext = with_halo(field, (("lat", 0),), 3, False)
    edge_rows = jnp.where(at_north, field[0:3], field[row_count - 3 : row_count])
    across = from_behind(edge_rows, "lon", lax.axis_size("lon") // 2)[::-1]
    upper = jnp.where(at_north, across, lat_ext[0:3])
    lower = jnp.where(at_south, across, lat_ext[row_count + 3 : row_count + 6])
    stacked = jnp.concatenate([upper, lat_ext[3 : row_count + 3], lower], axis=0)
    return with_halo(stacked, (("lon", 1),), 3, True)


CHAIN_ORDERS = (
    (("lat", 0), ("lon", 0), ("lon", 1), ("lat", 2), ("lat", 1), ("lon", 2), ("lat", 3), ("lon", 3)),
    (("lat", 0), ("lon", 1), ("lat", 2), ("lon", 0), ("lon", 2), ("lat", 1), ("lon", 3), ("lat", 3)),
)


def xor_partners(axis, bit):
    return [(j, j ^ (1 << bit)) for j in range(lax.axis_size(axis))]


def halve(buf, order):
    steps = []
    for axis, bit in order:
        side = (lax.axis_index(axis) >> bit) & 1
        half = buf.shape[0] // 2
        send = lax.dynamic_slice_in_dim(buf, (1 - side) * half, half, axis=0)
        keep = lax.dynamic_slice_in_dim(buf, side * half, half, axis=0)
        buf = keep + lax.ppermute(send, axis, xor_partners(axis, bit))
        steps.append((axis, bit, side))
    return buf, steps


def gather_back(buf, steps):
    for axis, bit, side in reversed(steps):
        other = lax.ppermute(buf, axis, xor_partners(axis, bit))
        low = jnp.where(side == 0, buf, other)
        high = jnp.where(side == 0, other, buf)
        buf = jnp.concatenate([low, high], axis=0)
    return buf.astype(jnp.float32)


def chained_sum(buf, halvings):
    count = len(CHAIN_ORDERS)
    rows = buf.shape[0] // count
    pieces = [halve(buf[c * rows : (c + 1) * rows], order[:halvings]) for c, order in enumerate(CHAIN_ORDERS)]
    joined = jnp.concatenate([piece for piece, _ in pieces], axis=0)
    for axis, bit in CHAIN_ORDERS[0][halvings:]:
        joined = joined + lax.ppermute(joined, axis, xor_partners(axis, bit))
    joined = joined.astype(jnp.bfloat16)
    size = joined.shape[0] // count
    return jnp.concatenate(
        [gather_back(joined[c * size : (c + 1) * size], steps) for c, (_, steps) in enumerate(pieces)],
        axis=0,
    )


def pack_terms(first, second):
    width = first[4].shape[1]
    big = jnp.concatenate([first[4], second[4], first[6], second[6]], axis=0)
    small = [piece.reshape(-1) for grads in (first, second) for i, piece in enumerate(grads) if i not in (4, 6)]
    flat = jnp.concatenate(small)
    rows = 32
    flat = jnp.pad(flat, (0, rows * width - flat.shape[0]))
    return jnp.concatenate([big, flat.reshape(rows, width)], axis=0)


def unpack_terms(buf, first, second):
    size = first[4].shape[0]
    big = buf[: 4 * size]
    flat = buf[4 * size :].reshape(-1)
    out = []
    offset = 0
    for b, grads in enumerate((first, second)):
        pieces = []
        for i, piece in enumerate(grads):
            if i == 4:
                pieces.append(big[b * size : (b + 1) * size])
            elif i == 6:
                pieces.append(big[(2 + b) * size : (3 + b) * size].T)
            else:
                pieces.append(flat[offset : offset + piece.size].reshape(piece.shape))
                offset = offset + piece.size
        out.append(tuple(pieces))
    return out


def per_device(
    inputs, grad_out, dw_kernel, dw_bias, ln_gain, ln_bias, w_up, b_up, w_down, b_down, layer_scale
):
    row_count, col_count, channels = inputs.shape
    at_north = lax.axis_index("lat") == 0
    at_south = lax.axis_index("lat") == lax.axis_size("lat") - 1
    cell_total = row_count * lax.axis_size("lat") * col_count * lax.axis_size("lon")

    def params(index):
        return (
            ln_gain[index],
            ln_bias[index],
            w_up[index],
            b_up[index],
            w_down[index],
            b_down[index],
            layer_scale[index],
        )

    def forward_block(index, field):
        extended = extend(field, at_north, at_south)
        conv_out = depthwise(extended, dw_kernel[index], row_count, col_count) + dw_bias[index]
        saved = cells_forward(conv_out.reshape(-1, channels), params(index))
        return (extended, saved)

    def backward_block(index, upstream, saved, extended):
        grad_cells, terms = cells_backward(upstream.reshape(-1, channels), saved, params(index))
        grad_cells = grad_cells.reshape(row_count, col_count, channels)
        kernel_term = kernel_grad(grad_cells, extended, row_count, col_count)
        bias_term = jnp.sum(grad_cells.astype(jnp.float32), axis=(0, 1))
        back = spread(
            extend(grad_cells, at_north, at_south),
            dw_kernel[index],
            row_count,
            col_count,
            at_north,
            at_south,
        )
        return (back, (kernel_term, bias_term) + terms)

    first_ext, first_saved = forward_block(0, inputs)
    middle = (
        inputs.reshape(-1, channels).astype(jnp.float32) + layer_scale[0] * first_saved[5]
    ).astype(jnp.bfloat16)
    middle = middle.reshape(row_count, col_count, channels)
    second_ext, second_saved = forward_block(1, middle)
    back_second, grads_second = backward_block(1, grad_out, second_saved, second_ext)
    upstream_first = (grad_out.astype(jnp.float32) + back_second).astype(jnp.bfloat16)
    back_first, grads_first = backward_block(0, upstream_first, first_saved, first_ext)
    grad_inputs = (upstream_first.astype(jnp.float32) + back_first).astype(jnp.bfloat16)
    packed = pack_terms(grads_first, grads_second)
    summed = chained_sum(packed, 4)
    grads_first, grads_second = unpack_terms(summed, grads_first, grads_second)
    inv_root = 1.0 / math.sqrt(cell_total)
    joined = [jnp.stack([grads_first[slot], grads_second[slot]]) * inv_root for slot in range(9)]
    return (
        grad_inputs,
        joined[0],
        joined[1],
        joined[2],
        joined[3],
        joined[4],
        joined[5],
        joined[6],
        joined[7],
        joined[8],
    )


def solution(mesh):
    placed = (
        P("lat", "lon", None),
        P("lat", "lon", None),
        P(),
        P(),
        P(),
        P(),
        P(),
        P(),
        P(),
        P(),
        P(),
    )
    return jax.shard_map(
        per_device,
        mesh=mesh,
        in_specs=placed,
        out_specs=(P("lat", "lon", None), P(), P(), P(), P(), P(), P(), P(), P(), P()),
        check_vma=False,
    )
```

```python
import math

import jax
import jax.numpy as jnp
from jax import lax
from jax.sharding import PartitionSpec as P

EPS = 1e-06
ROOT_TWO_PI = math.sqrt(2.0 / math.pi)
CUBIC = 0.044715


def with_halo(cells, sides, width, closed):
    for axis, dim in sides:
        count = lax.axis_size(axis)
        ends = count if closed else count - 1
        head = lax.slice_in_dim(cells, 0, width, axis=dim)
        tail = lax.slice_in_dim(cells, cells.shape[dim] - width, cells.shape[dim], axis=dim)
        cells = jnp.concatenate(
            [
                lax.ppermute(tail, axis, [(i, (i + 1) % count) for i in range(ends)]),
                cells,
                lax.ppermute(head, axis, [((i + 1) % count, i) for i in range(ends)]),
            ],
            axis=dim,
        )
    return cells


def from_behind(block, axis, distance):
    devices = range(lax.axis_size(axis))
    route = [((i - distance) % len(devices), i) for i in devices]
    return lax.ppermute(block, axis, route)


def gelu_pair(hidden):
    inner = ROOT_TWO_PI * (hidden + CUBIC * hidden * hidden * hidden)
    tanh_val = jnp.tanh(inner)
    value = 0.5 * hidden * (1.0 + tanh_val)
    slope = 0.5 * (1.0 + tanh_val) + 0.5 * hidden * (1.0 - tanh_val * tanh_val) * ROOT_TWO_PI * (
        1.0 + 3.0 * CUBIC * hidden * hidden
    )
    return (value, slope)


def depthwise(extended, kernel, row_count, col_count):
    total = jnp.zeros((row_count, col_count, extended.shape[2]), jnp.float32)
    for tap_row in range(7):
        for tap_col in range(7):
            window = extended[tap_row : tap_row + row_count, tap_col : tap_col + col_count].astype(
                jnp.float32
            )
            total = total + window * kernel[tap_row, tap_col]
    return total


def kernel_grad(grad_cells, extended, row_count, col_count):
    grad_float = grad_cells.astype(jnp.float32)
    rows_out = []
    for tap_row in range(7):
        row_terms = []
        for tap_col in range(7):
            window = extended[tap_row : tap_row + row_count, tap_col : tap_col + col_count].astype(
                jnp.float32
            )
            row_terms.append(jnp.sum(grad_float * window, axis=(0, 1)))
        rows_out.append(jnp.stack(row_terms))
    return jnp.stack(rows_out)


def spread(extended_grad, kernel, row_count, col_count, at_north, at_south):
    row_ids = jnp.arange(row_count + 6)[:, None, None]
    north_mask = jnp.logical_and(at_north, row_ids < 3)
    south_mask = jnp.logical_and(at_south, row_ids >= row_count + 3)
    polar = jnp.logical_or(north_mask, south_mask)
    zeros = jnp.zeros_like(extended_grad)
    normal = jnp.where(polar, zeros, extended_grad)
    north_part = jnp.where(north_mask, extended_grad, zeros)
    south_part = jnp.where(south_mask, extended_grad, zeros)
    result = depthwise(normal, kernel[::-1, ::-1], row_count, col_count)
    upper = depthwise(north_part[0:9], kernel[:, ::-1], 3, col_count)
    lower = depthwise(south_part[row_count - 3 : row_count + 6], kernel[:, ::-1], 3, col_count)
    result = result.at[0:3].add(upper)
    return result.at[row_count - 3 : row_count].add(lower)


def cells_forward(conv_cells, params):
    gain, shift_ln, weight_up, bias_up, weight_down, bias_down, branch_scale = params
    ch_mean = jnp.mean(conv_cells, axis=-1, keepdims=True)
    centred = conv_cells - ch_mean
    ch_var = jnp.mean(centred * centred, axis=-1, keepdims=True)
    inv_std = lax.rsqrt(ch_var + EPS)
    normal_x = centred * inv_std
    normed = (normal_x * gain + shift_ln).astype(jnp.bfloat16)
    hidden = jnp.dot(normed, weight_up, preferred_element_type=jnp.float32) + bias_up
    value, slope = gelu_pair(hidden)
    activ = value.astype(jnp.bfloat16)
    branch = jnp.dot(activ, weight_down, preferred_element_type=jnp.float32) + bias_down
    return (normed, normal_x, inv_std, activ, slope, branch)


def cells_backward(upstream, saved, params):
    normed, normal_x, inv_std, activ, slope, branch = saved
    gain, shift_ln, weight_up, bias_up, weight_down, bias_down, branch_scale = params
    up_float = upstream.astype(jnp.float32)
    d_scale = jnp.sum(up_float * branch, axis=0)
    grad_branch = (up_float * branch_scale).astype(jnp.bfloat16)
    d_bias_down = jnp.sum(grad_branch.astype(jnp.float32), axis=0)
    d_weight_down = jnp.dot(grad_branch.T, activ, preferred_element_type=jnp.float32)
    grad_activ = jnp.dot(grad_branch, weight_down.T, preferred_element_type=jnp.float32)
    grad_hidden = (grad_activ * slope).astype(jnp.bfloat16)
    d_bias_up = jnp.sum(grad_hidden.astype(jnp.float32), axis=0)
    d_weight_up = jnp.dot(normed.T, grad_hidden, preferred_element_type=jnp.float32)
    grad_normed = jnp.dot(grad_hidden, weight_up.T, preferred_element_type=jnp.float32)
    d_gain = jnp.sum(grad_normed * normal_x, axis=0)
    d_shift = jnp.sum(grad_normed, axis=0)
    scaled = grad_normed * gain
    grad_conv = inv_std * (
        scaled
        - jnp.mean(scaled, axis=-1, keepdims=True)
        - normal_x * jnp.mean(scaled * normal_x, axis=-1, keepdims=True)
    )
    return (
        grad_conv.astype(jnp.bfloat16),
        (d_gain, d_shift, d_weight_up, d_bias_up, d_weight_down, d_bias_down, d_scale),
    )


def extend(field, at_north, at_south):
    row_count = field.shape[0]
    lat_ext = with_halo(field, (("lat", 0),), 3, False)
    edge_rows = jnp.where(at_north, field[0:3], field[row_count - 3 : row_count])
    across = from_behind(edge_rows, "lon", lax.axis_size("lon") // 2)[::-1]
    upper = jnp.where(at_north, across, lat_ext[0:3])
    lower = jnp.where(at_south, across, lat_ext[row_count + 3 : row_count + 6])
    stacked = jnp.concatenate([upper, lat_ext[3 : row_count + 3], lower], axis=0)
    return with_halo(stacked, (("lon", 1),), 3, True)


CHAIN_ORDERS = (
    (("lat", 0), ("lon", 0), ("lon", 1), ("lat", 2), ("lat", 1), ("lon", 2), ("lat", 3), ("lon", 3)),
    (("lat", 0), ("lon", 1), ("lat", 2), ("lon", 0), ("lon", 2), ("lat", 1), ("lon", 3), ("lat", 3)),
)


def xor_partners(axis, bit):
    return [(j, j ^ (1 << bit)) for j in range(lax.axis_size(axis))]


def halve(buf, order):
    steps = []
    for axis, bit in order:
        side = (lax.axis_index(axis) >> bit) & 1
        half = buf.shape[0] // 2
        send = lax.dynamic_slice_in_dim(buf, (1 - side) * half, half, axis=0)
        keep = lax.dynamic_slice_in_dim(buf, side * half, half, axis=0)
        buf = keep + lax.ppermute(send, axis, xor_partners(axis, bit))
        steps.append((axis, bit, side))
    return buf, steps


def gather_back(buf, steps):
    for axis, bit, side in reversed(steps):
        other = lax.ppermute(buf, axis, xor_partners(axis, bit))
        low = jnp.where(side == 0, buf, other)
        high = jnp.where(side == 0, other, buf)
        buf = jnp.concatenate([low, high], axis=0)
    return buf


def chained_sum(buf, halvings):
    count = len(CHAIN_ORDERS)
    buf, shared = halve(buf, CHAIN_ORDERS[0][:1])
    rows = buf.shape[0] // count
    pieces = [halve(buf[c * rows : (c + 1) * rows], order[1:halvings]) for c, order in enumerate(CHAIN_ORDERS)]
    joined = jnp.concatenate([piece for piece, _ in pieces], axis=0)
    for axis, bit in CHAIN_ORDERS[0][halvings:]:
        joined = joined + lax.ppermute(joined, axis, xor_partners(axis, bit))
    joined = joined.astype(jnp.bfloat16)
    size = joined.shape[0] // count
    joined = jnp.concatenate(
        [gather_back(joined[c * size : (c + 1) * size], steps) for c, (_, steps) in enumerate(pieces)],
        axis=0,
    )
    return gather_back(joined, shared).astype(jnp.float32)


def pack_terms(first, second):
    width = first[4].shape[1]
    big = jnp.concatenate([first[4], second[4], first[6], second[6]], axis=0)
    small = [piece.reshape(-1) for grads in (first, second) for i, piece in enumerate(grads) if i not in (4, 6)]
    flat = jnp.concatenate(small)
    rows = 32
    flat = jnp.pad(flat, (0, rows * width - flat.shape[0]))
    return jnp.concatenate([big, flat.reshape(rows, width)], axis=0)


def unpack_terms(buf, first, second):
    size = first[4].shape[0]
    big = buf[: 4 * size]
    flat = buf[4 * size :].reshape(-1)
    out = []
    offset = 0
    for b, grads in enumerate((first, second)):
        pieces = []
        for i, piece in enumerate(grads):
            if i == 4:
                pieces.append(big[b * size : (b + 1) * size])
            elif i == 6:
                pieces.append(big[(2 + b) * size : (3 + b) * size].T)
            else:
                pieces.append(flat[offset : offset + piece.size].reshape(piece.shape))
                offset = offset + piece.size
        out.append(tuple(pieces))
    return out


def per_device(
    inputs, grad_out, dw_kernel, dw_bias, ln_gain, ln_bias, w_up, b_up, w_down, b_down, layer_scale
):
    row_count, col_count, channels = inputs.shape
    at_north = lax.axis_index("lat") == 0
    at_south = lax.axis_index("lat") == lax.axis_size("lat") - 1
    cell_total = row_count * lax.axis_size("lat") * col_count * lax.axis_size("lon")

    def params(index):
        return (
            ln_gain[index],
            ln_bias[index],
            w_up[index],
            b_up[index],
            w_down[index],
            b_down[index],
            layer_scale[index],
        )

    def forward_block(index, field):
        extended = extend(field, at_north, at_south)
        conv_out = depthwise(extended, dw_kernel[index], row_count, col_count) + dw_bias[index]
        saved = cells_forward(conv_out.reshape(-1, channels), params(index))
        return (extended, saved)

    def backward_block(index, upstream, saved, extended):
        grad_cells, terms = cells_backward(upstream.reshape(-1, channels), saved, params(index))
        grad_cells = grad_cells.reshape(row_count, col_count, channels)
        kernel_term = kernel_grad(grad_cells, extended, row_count, col_count)
        bias_term = jnp.sum(grad_cells.astype(jnp.float32), axis=(0, 1))
        back = spread(
            extend(grad_cells, at_north, at_south),
            dw_kernel[index],
            row_count,
            col_count,
            at_north,
            at_south,
        )
        return (back, (kernel_term, bias_term) + terms)

    first_ext, first_saved = forward_block(0, inputs)
    middle = (
        inputs.reshape(-1, channels).astype(jnp.float32) + layer_scale[0] * first_saved[5]
    ).astype(jnp.bfloat16)
    middle = middle.reshape(row_count, col_count, channels)
    second_ext, second_saved = forward_block(1, middle)
    back_second, grads_second = backward_block(1, grad_out, second_saved, second_ext)
    upstream_first = (grad_out.astype(jnp.float32) + back_second).astype(jnp.bfloat16)
    back_first, grads_first = backward_block(0, upstream_first, first_saved, first_ext)
    grad_inputs = (upstream_first.astype(jnp.float32) + back_first).astype(jnp.bfloat16)
    packed = pack_terms(grads_first, grads_second)
    summed = chained_sum(packed, 4)
    grads_first, grads_second = unpack_terms(summed, grads_first, grads_second)
    inv_root = 1.0 / math.sqrt(cell_total)
    joined = [jnp.stack([grads_first[slot], grads_second[slot]]) * inv_root for slot in range(9)]
    return (
        grad_inputs,
        joined[0],
        joined[1],
        joined[2],
        joined[3],
        joined[4],
        joined[5],
        joined[6],
        joined[7],
        joined[8],
    )


def solution(mesh):
    placed = (
        P("lat", "lon", None),
        P("lat", "lon", None),
        P(),
        P(),
        P(),
        P(),
        P(),
        P(),
        P(),
        P(),
        P(),
    )
    return jax.shard_map(
        per_device,
        mesh=mesh,
        in_specs=placed,
        out_specs=(P("lat", "lon", None), P(), P(), P(), P(), P(), P(), P(), P(), P()),
        check_vma=False,
    )
```
